128 devices in a mesh: rep: 4 (over z), shard: 32 (over x, y, core).
Axes of the slice: x: 4, y: 4, z: 4, core: 2. Of those that a mesh axis runs over, the one named last changes fastest.
Arguments:
- trained_sq: float32 [4, 4, 768, 768], P('rep', None, 'shard'), may hold values from -6 to 6
- trained_up: float32 [4, 768, 3072], P('rep', 'shard'), may hold values from -6 to 6
- trained_down: float32 [4, 3072, 768], P('rep', 'shard'), may hold values from -6 to 6
- trained_ln: float32 [4, 4, 768], P('rep', None, 'shard'), may hold values from -6 to 6
- start_sq: float32 [4, 768, 768], P(None, 'shard'), may hold values from -6 to 6
- start_up: float32 [768, 3072], P('shard'), may hold values from -6 to 6
- start_down: float32 [3072, 768], P('shard'), may hold values from -6 to 6
- start_ln: float32 [4, 768], P(None, 'shard'), may hold values from -6 to 6
- resid_sq: float32 [4, 4, 768, 768], P('rep', None, 'shard'), may hold values from -4 to 4
- resid_up: float32 [4, 768, 3072], P('rep', 'shard'), may hold values from -4 to 4
- resid_down: float32 [4, 3072, 768], P('rep', 'shard'), may hold values from -4 to 4
- mom_sq: float32 [4, 768, 768], P(None, 'shard'), may hold values from -3 to 3
- mom_up: float32 [768, 3072], P('shard'), may hold values from -3 to 3
- mom_down: float32 [3072, 768], P('shard'), may hold values from -3 to 3
- mom_ln: float32 [4, 768], P(None, 'shard'), may hold values from -3 to 3
- basis_sq: float32 [4, 768, 64], replicated, may hold values from -0.21875 to 0.21875
- basis_up: float32 [3072, 64], replicated, may hold values from -0.109375 to 0.109375
- basis_down: float32 [768, 64], replicated, may hold values from -0.21875 to 0.21875
Outputs:
- new_resid_sq: float32 [4, 4, 768, 768], P('rep', None, 'shard')
- new_resid_up: float32 [4, 768, 3072], P('rep', 'shard')
- new_resid_down: float32 [4, 3072, 768], P('rep', 'shard')
- new_mom_sq: float32 [4, 768, 768], P(None, 'shard')
- new_mom_up: float32 [768, 3072], P('shard')
- new_mom_down: float32 [3072, 768], P('shard')
- new_mom_ln: float32 [4, 768], P(None, 'shard')
- weights_sq: bfloat16 [4, 768, 768], replicated
- weights_up: bfloat16 [768, 3072], replicated
- weights_down: bfloat16 [3072, 768], replicated
- weights_ln: bfloat16 [4, 768], replicated
The draws below stay inside these ranges and needn't reach their ends.
All inputs are finite; a program needn't handle non-finite values.
Results may differ from the reference program's by a relative error of at most 0.001.
Values may be sent and summed in bfloat16 or wider, within the bound.
No kernel may reach another device: no remote copies, remote signals or barrier semaphores. Data moves between devices by JAX's collectives and lax.ppermute only.
A program may use at most 128 MiB of HBM per device.

```python
import jax
import jax.numpy as jnp
from jax import lax

D = 768
FF = 3072
RANK = 64
SQUARE = 4
GROUPS = 4


def levels(stream_key, shape, cuts, smallest, top_value):
    gain, own = 1.0, jax.random.fold_in(stream_key, 6)
    for dim, blocks in cuts:
        steps = jnp.exp(jax.random.uniform(jax.random.fold_in(own, dim), (blocks,), jnp.float32, smallest / len(cuts), top_value / len(cuts)))
        gain = gain * jnp.repeat(steps, shape[dim] // blocks).reshape([-1 if axis == dim else 1 for axis in range(len(shape))])
    return gain


def scatter_about(key, dims, deviation, bound, shards=(), held_as=jnp.bfloat16):
    array = deviation * jax.random.normal(key, dims, jnp.float32)
    if shards:
        array = array * levels(key, dims, shards, -0.22, 0.18)
    return jnp.clip(array, -bound, bound).astype(held_as)


def setup_inputs(seed: int = 0) -> dict:
    key_of = jax.random.split(jax.random.key(seed), 19)
    return {
        "trained_sq": scatter_about(key_of[0], (GROUPS, SQUARE, D, D), 1.0, 6.0, ((0, 4), (2, 32)), jnp.float32),
        "trained_up": scatter_about(key_of[1], (GROUPS, D, FF), 1.0, 6.0, ((0, 4), (1, 32)), jnp.float32),
        "trained_down": scatter_about(key_of[2], (GROUPS, FF, D), 1.0, 6.0, ((0, 4), (1, 32)), jnp.float32),
        "trained_ln": scatter_about(key_of[3], (GROUPS, 4, D), 1.0, 6.0, ((0, 4), (2, 32)), jnp.float32),
        "start_sq": scatter_about(key_of[4], (SQUARE, D, D), 1.0, 6.0, ((1, 32),), jnp.float32),
        "start_up": scatter_about(key_of[5], (D, FF), 1.0, 6.0, ((0, 32),), jnp.float32),
        "start_down": scatter_about(key_of[6], (FF, D), 1.0, 6.0, ((0, 32),), jnp.float32),
        "start_ln": scatter_about(key_of[7], (4, D), 1.0, 6.0, ((1, 32),), jnp.float32),
        "resid_sq": scatter_about(key_of[8], (GROUPS, SQUARE, D, D), 0.5, 4.0, ((0, 4), (2, 32)), jnp.float32),
        "resid_up": scatter_about(key_of[9], (GROUPS, D, FF), 0.5, 4.0, ((0, 4), (1, 32)), jnp.float32),
        "resid_down": scatter_about(key_of[10], (GROUPS, FF, D), 0.5, 4.0, ((0, 4), (1, 32)), jnp.float32),
        "mom_sq": scatter_about(key_of[11], (SQUARE, D, D), 0.3, 3.0, ((1, 32),), jnp.float32),
        "mom_up": scatter_about(key_of[12], (D, FF), 0.3, 3.0, ((0, 32),), jnp.float32),
        "mom_down": scatter_about(key_of[13], (FF, D), 0.3, 3.0, ((0, 32),), jnp.float32),
        "mom_ln": scatter_about(key_of[14], (4, D), 0.3, 3.0, ((1, 32),), jnp.float32),
        "basis_sq": scatter_about(key_of[15], (SQUARE, D, RANK), D ** -0.5, 0.21875, (), jnp.float32),
        "basis_up": scatter_about(key_of[16], (FF, RANK), FF ** -0.5, 0.109375, (), jnp.float32),
        "basis_down": scatter_about(key_of[17], (D, RANK), D ** -0.5, 0.21875, (), jnp.float32),
    }


moment_coef = 0.9
outer_rate = 0.7


def advance(start, moment, outer):
    new_moment = moment_coef * moment + outer
    weights = (start - outer_rate * (outer + moment_coef * new_moment)).astype(jnp.bfloat16)
    return new_moment, weights


def reference(trained_sq, trained_up, trained_down, trained_ln, start_sq, start_up, start_down, start_ln, resid_sq, resid_up, resid_down, mom_sq, mom_up, mom_down, mom_ln, basis_sq, basis_up, basis_down):
    highest = lax.Precision.HIGHEST
    delta_sq = start_sq[None] - trained_sq + resid_sq
    factor_sq = jnp.einsum("gmrd,mdk->gmrk", delta_sq, basis_sq, precision=highest)
    new_resid_sq = delta_sq - jnp.einsum("gmrk,mdk->gmrd", factor_sq, basis_sq, precision=highest)
    delta_up = start_up[None] - trained_up + resid_up
    factor_up = jnp.einsum("grf,fk->grk", delta_up, basis_up, precision=highest)
    new_resid_up = delta_up - jnp.einsum("grk,fk->grf", factor_up, basis_up, precision=highest)
    delta_down = start_down[None] - trained_down + resid_down
    factor_down = jnp.einsum("grd,dk->grk", delta_down, basis_down, precision=highest)
    new_resid_down = delta_down - jnp.einsum("grk,dk->grd", factor_down, basis_down, precision=highest)
    mean_sq = jnp.sum(factor_sq, axis=0) / GROUPS
    mean_up = jnp.sum(factor_up, axis=0) / GROUPS
    mean_down = jnp.sum(factor_down, axis=0) / GROUPS
    mean_ln = jnp.sum(start_ln[None] - trained_ln, axis=0) / GROUPS
    outer_sq = jnp.einsum("mrk,mdk->mrd", mean_sq, basis_sq, precision=highest)
    outer_up = jnp.einsum("rk,fk->rf", mean_up, basis_up, precision=highest)
    outer_down = jnp.einsum("rk,dk->rd", mean_down, basis_down, precision=highest)
    new_mom_sq, weights_sq = advance(start_sq, mom_sq, outer_sq)
    new_mom_up, weights_up = advance(start_up, mom_up, outer_up)
    new_mom_down, weights_down = advance(start_down, mom_down, outer_down)
    new_mom_ln, weights_ln = advance(start_ln, mom_ln, mean_ln)
    return (new_resid_sq, new_resid_up, new_resid_down, new_mom_sq, new_mom_up, new_mom_down, new_mom_ln, weights_sq, weights_up, weights_down, weights_ln)
```

```python
import jax
import jax.numpy as jnp
from jax import lax
from jax.sharding import PartitionSpec as P

moment_coef = 0.9
outer_rate = 0.7


def advance(start, moment, outer):
    new_moment = moment_coef * moment + outer
    weights = (start - outer_rate * (outer + moment_coef * new_moment)).astype(jnp.bfloat16)
    return (new_moment, weights)


def split_cols(a, width):
    return a.reshape(a.shape[0], -1, width).transpose(1, 0, 2)


def join_cols(a):
    return a.transpose(1, 0, 2).reshape(a.shape[1], -1)


def on_device(
    trained_sq,
    trained_up,
    trained_down,
    trained_ln,
    start_sq,
    start_up,
    start_down,
    start_ln,
    resid_sq,
    resid_up,
    resid_down,
    mom_sq,
    mom_up,
    mom_down,
    mom_ln,
    basis_sq,
    basis_up,
    basis_down,
):
    highest = lax.Precision.HIGHEST
    groups = lax.axis_size("rep")
    square, rows, width = start_sq.shape
    rank = basis_sq.shape[-1]
    delta_sq = start_sq - trained_sq[0] + resid_sq[0]
    factor_sq = jnp.einsum("mrd,mdk->mrk", delta_sq, basis_sq, precision=highest)
    new_resid_sq = delta_sq - jnp.einsum("mrk,mdk->mrd", factor_sq, basis_sq, precision=highest)
    delta_up = start_up - trained_up[0] + resid_up[0]
    factor_up = jnp.dot(delta_up, basis_up, precision=highest, preferred_element_type=jnp.float32)
    new_resid_up = delta_up - jnp.einsum("rk,fk->rf", factor_up, basis_up, precision=highest)
    delta_down = start_down - trained_down[0] + resid_down[0]
    factor_down = jnp.dot(
        delta_down, basis_down, precision=highest, preferred_element_type=jnp.float32
    )
    new_resid_down = delta_down - jnp.einsum(
        "rk,dk->rd", factor_down, basis_down, precision=highest
    )
    norm_delta = start_ln - trained_ln[0]
    summed = lax.psum((factor_sq, factor_up, factor_down, norm_delta), "rep")
    mean_sq = summed[0] / groups
    mean_up = summed[1] / groups
    mean_down = summed[2] / groups
    mean_ln = summed[3] / groups
    new_mom_ln, norm_weights = advance(start_ln, mom_ln, mean_ln)
    blocks_up = start_up.shape[1] // width
    blocks_down = start_down.shape[0] // rows
    start_all = jnp.concatenate(
        [start_sq, split_cols(start_up, width), start_down.reshape(blocks_down, rows, width)]
    )
    mom_all = jnp.concatenate(
        [mom_sq, split_cols(mom_up, width), mom_down.reshape(blocks_down, rows, width)]
    )
    mean_all = jnp.concatenate(
        [
            mean_sq,
            jnp.broadcast_to(mean_up[None], (blocks_up, rows, rank)),
            mean_down.reshape(blocks_down, rows, rank),
        ]
    )
    basis_all = jnp.concatenate(
        [
            basis_sq,
            basis_up.reshape(blocks_up, width, rank),
            jnp.broadcast_to(basis_down[None], (blocks_down, width, rank)),
        ]
    )
    outer_all = jnp.einsum("brk,bdk->brd", mean_all, basis_all, precision=highest)
    new_mom_all, owned_all = advance(start_all, mom_all, outer_all)
    new_mom_sq = new_mom_all[:square]
    new_mom_up = join_cols(new_mom_all[square : square + blocks_up])
    new_mom_down = new_mom_all[square + blocks_up :].reshape(-1, width)
    gathered = lax.all_gather(owned_all, "shard", axis=1, tiled=True)
    shards = lax.axis_size("shard")
    weights_sq = gathered[:square]
    weights_up = join_cols(gathered[square : square + blocks_up])
    down = gathered[square + blocks_up :].reshape(blocks_down, shards, rows, width)
    weights_down = down.transpose(1, 0, 2, 3).reshape(-1, width)
    weights_ln = lax.all_gather(norm_weights, "shard", axis=1, tiled=True)
    return (
        new_resid_sq[None],
        new_resid_up[None],
        new_resid_down[None],
        new_mom_sq,
        new_mom_up,
        new_mom_down,
        new_mom_ln,
        weights_sq,
        weights_up,
        weights_down,
        weights_ln,
    )


def solution(mesh):
    placed = (
        P("rep", None, "shard", None),
        P("rep", "shard", None),
        P("rep", "shard", None),
        P("rep", None, "shard"),
        P(None, "shard", None),
        P("shard", None),
        P("shard", None),
        P(None, "shard"),
        P("rep", None, "shard", None),
        P("rep", "shard", None),
        P("rep", "shard", None),
        P(None, "shard", None),
        P("shard", None),
        P("shard", None),
        P(None, "shard"),
        P(),
        P(),
        P(),
    )
    return jax.shard_map(
        on_device,
        mesh=mesh,
        in_specs=placed,
        out_specs=(
            P("rep", None, "shard", None),
            P("rep", "shard", None),
            P("rep", "shard", None),
            P(None, "shard", None),
            P("shard", None),
            P("shard", None),
            P(None, "shard"),
            P(),
            P(),
            P(),
            P(),
        ),
        check_vma=False,
    )
```

```python
import jax
import jax.numpy as jnp
from jax import lax
from jax.experimental import pallas as pl
from jax.sharding import PartitionSpec as P

moment_coef = 0.9
outer_rate = 0.7


def advance(start, moment, outer):
    new_moment = moment_coef * moment + outer
    weights = (start - outer_rate * (outer + moment_coef * new_moment)).astype(jnp.bfloat16)
    return (new_moment, weights)


def split_cols(a, width):
    return a.reshape(a.shape[0], -1, width).transpose(1, 0, 2)


def join_cols(a):
    return a.transpose(1, 0, 2).reshape(a.shape[1], -1)


def unpack_kernel(g_ref, sq_ref, up_ref, down_ref):
    blocks = g_ref.shape[1]
    rows = g_ref.shape[2] // 2
    sq_ref[...] = g_ref[0]
    up_ref[...] = jnp.concatenate([g_ref[1, k] for k in range(blocks)], axis=1)
    x = g_ref[2].astype(jnp.float32)
    pieces = [x[q, h * rows : (h + 1) * rows] for h in range(2) for q in range(blocks)]
    down_ref[...] = jnp.concatenate(pieces, axis=0).astype(down_ref.dtype)


def unpack(gathered, rows):
    kinds_blocks, total, width = gathered.shape
    blocks = kinds_blocks // 3
    g = gathered.reshape(3, blocks, total, width)
    step = 2 * rows
    dt = gathered.dtype
    nbytes = 2 * gathered.size * dt.itemsize
    return pl.pallas_call(
        unpack_kernel,
        grid=(total // step,),
        in_specs=[pl.BlockSpec((3, blocks, step, width), lambda j: (0, 0, j, 0))],
        out_specs=[
            pl.BlockSpec((blocks, step, width), lambda j: (0, j, 0)),
            pl.BlockSpec((step, blocks * width), lambda j: (j, 0)),
            pl.BlockSpec((blocks * step, width), lambda j: (j, 0)),
        ],
        out_shape=[
            jax.ShapeDtypeStruct((blocks, total, width), dt),
            jax.ShapeDtypeStruct((total, blocks * width), dt),
            jax.ShapeDtypeStruct((blocks * total, width), dt),
        ],
        cost_estimate=pl.CostEstimate(flops=0, transcendentals=0, bytes_accessed=nbytes),
    )(g)


def on_device(
    trained_sq,
    trained_up,
    trained_down,
    trained_ln,
    start_sq,
    start_up,
    start_down,
    start_ln,
    resid_sq,
    resid_up,
    resid_down,
    mom_sq,
    mom_up,
    mom_down,
    mom_ln,
    basis_sq,
    basis_up,
    basis_down,
):
    highest = lax.Precision.HIGHEST
    groups = lax.axis_size("rep")
    square, rows, width = start_sq.shape
    rank = basis_sq.shape[-1]
    delta_sq = start_sq - trained_sq[0] + resid_sq[0]
    factor_sq = jnp.einsum("mrd,mdk->mrk", delta_sq, basis_sq, precision=highest)
    new_resid_sq = delta_sq - jnp.einsum("mrk,mdk->mrd", factor_sq, basis_sq, precision=highest)
    delta_up = start_up - trained_up[0] + resid_up[0]
    factor_up = jnp.dot(delta_up, basis_up, precision=highest, preferred_element_type=jnp.float32)
    new_resid_up = delta_up - jnp.einsum("rk,fk->rf", factor_up, basis_up, precision=highest)
    delta_down = start_down - trained_down[0] + resid_down[0]
    factor_down = jnp.dot(
        delta_down, basis_down, precision=highest, preferred_element_type=jnp.float32
    )
    new_resid_down = delta_down - jnp.einsum(
        "rk,dk->rd", factor_down, basis_down, precision=highest
    )
    norm_delta = start_ln - trained_ln[0]
    summed = lax.psum((factor_sq, factor_up, factor_down, norm_delta), "rep")
    mean_sq = summed[0] / groups
    mean_up = summed[1] / groups
    mean_down = summed[2] / groups
    mean_ln = summed[3] / groups
    new_mom_ln, norm_weights = advance(start_ln, mom_ln, mean_ln)
    blocks_up = start_up.shape[1] // width
    blocks_down = start_down.shape[0] // rows
    start_all = jnp.concatenate(
        [start_sq, split_cols(start_up, width), start_down.reshape(blocks_down, rows, width)]
    )
    mom_all = jnp.concatenate(
        [mom_sq, split_cols(mom_up, width), mom_down.reshape(blocks_down, rows, width)]
    )
    mean_all = jnp.concatenate(
        [
            mean_sq,
            jnp.broadcast_to(mean_up[None], (blocks_up, rows, rank)),
            mean_down.reshape(blocks_down, rows, rank),
        ]
    )
    basis_all = jnp.concatenate(
        [
            basis_sq,
            basis_up.reshape(blocks_up, width, rank),
            jnp.broadcast_to(basis_down[None], (blocks_down, width, rank)),
        ]
    )
    outer_all = jnp.einsum("brk,bdk->brd", mean_all, basis_all, precision=highest)
    new_mom_all, owned_all = advance(start_all, mom_all, outer_all)
    new_mom_sq = new_mom_all[:square]
    new_mom_up = join_cols(new_mom_all[square : square + blocks_up])
    new_mom_down = new_mom_all[square + blocks_up :].reshape(-1, width)
    gathered = lax.all_gather(owned_all, "shard", axis=1, tiled=True)
    weights_sq, weights_up, weights_down = unpack(gathered, rows)
    weights_ln = lax.all_gather(norm_weights, "shard", axis=1, tiled=True)
    return (
        new_resid_sq[None],
        new_resid_up[None],
        new_resid_down[None],
        new_mom_sq,
        new_mom_up,
        new_mom_down,
        new_mom_ln,
        weights_sq,
        weights_up,
        weights_down,
        weights_ln,
    )


def solution(mesh):
    placed = (
        P("rep", None, "shard", None),
        P("rep", "shard", None),
        P("rep", "shard", None),
        P("rep", None, "shard"),
        P(None, "shard", None),
        P("shard", None),
        P("shard", None),
        P(None, "shard"),
        P("rep", None, "shard", None),
        P("rep", "shard", None),
        P("rep", "shard", None),
        P(None, "shard", None),
        P("shard", None),
        P("shard", None),
        P(None, "shard"),
        P(),
        P(),
        P(),
    )
    return jax.shard_map(
        on_device,
        mesh=mesh,
        in_specs=placed,
        out_specs=(
            P("rep", None, "shard", None),
            P("rep", "shard", None),
            P("rep", "shard", None),
            P(None, "shard", None),
            P("shard", None),
            P("shard", None),
            P(None, "shard"),
            P(),
            P(),
            P(),
            P(),
        ),
        check_vma=False,
    )
```

```python
import functools

import jax
import jax.numpy as jnp
from jax import lax
from jax.experimental import pallas as pl
from jax.sharding import PartitionSpec as P

moment_coef = 0.9
outer_rate = 0.7


def advance(start, moment, outer):
    new_moment = moment_coef * moment + outer
    weights = (start - outer_rate * (outer + moment_coef * new_moment)).astype(jnp.bfloat16)
    return (new_moment, weights)


def split_cols(a, width):
    return a.reshape(a.shape[0], -1, width).transpose(1, 0, 2)


def join_cols(a):
    return a.transpose(1, 0, 2).reshape(a.shape[1], -1)


def unpack_kernel(rows, g_ref, sq_ref, up_ref, down_ref):
    blocks = g_ref.shape[1]
    sq_ref[...] = g_ref[0]
    up_ref[...] = jnp.concatenate([g_ref[1, k] for k in range(blocks)], axis=1)
    x = g_ref[2].astype(jnp.float32)
    per_step = g_ref.shape[2] // rows
    pieces = [x[q, h * rows : (h + 1) * rows] for h in range(per_step) for q in range(blocks)]
    down_ref[...] = jnp.concatenate(pieces, axis=0).astype(down_ref.dtype)


def unpack(gathered, rows):
    kinds_blocks, total, width = gathered.shape
    blocks = kinds_blocks // 3
    g = gathered.reshape(3, blocks, total, width)
    step = 8 * rows
    dt = gathered.dtype
    nbytes = 2 * gathered.size * dt.itemsize
    return pl.pallas_call(
        functools.partial(unpack_kernel, rows),
        grid=(total // step,),
        in_specs=[pl.BlockSpec((3, blocks, step, width), lambda j: (0, 0, j, 0))],
        out_specs=[
            pl.BlockSpec((blocks, step, width), lambda j: (0, j, 0)),
            pl.BlockSpec((step, blocks * width), lambda j: (j, 0)),
            pl.BlockSpec((blocks * step, width), lambda j: (j, 0)),
        ],
        out_shape=[
            jax.ShapeDtypeStruct((blocks, total, width), dt),
            jax.ShapeDtypeStruct((total, blocks * width), dt),
            jax.ShapeDtypeStruct((blocks * total, width), dt),
        ],
        cost_estimate=pl.CostEstimate(flops=0, transcendentals=0, bytes_accessed=nbytes),
    )(g)


def rep_sum(parts):
    n = lax.axis_size("rep")
    step = 1
    while step < n:
        other = lax.ppermute(parts, "rep", [(i, i ^ step) for i in range(n)])
        parts = jax.tree.map(jnp.add, parts, other)
        step *= 2
    return parts


def on_device(
    trained_sq,
    trained_up,
    trained_down,
    trained_ln,
    start_sq,
    start_up,
    start_down,
    start_ln,
    resid_sq,
    resid_up,
    resid_down,
    mom_sq,
    mom_up,
    mom_down,
    mom_ln,
    basis_sq,
    basis_up,
    basis_down,
):
    highest = lax.Precision.HIGHEST
    groups = lax.axis_size("rep")
    square, rows, width = start_sq.shape
    rank = basis_sq.shape[-1]
    delta_sq = start_sq - trained_sq[0] + resid_sq[0]
    factor_sq = jnp.einsum("mrd,mdk->mrk", delta_sq, basis_sq, precision=highest)
    new_resid_sq = delta_sq - jnp.einsum("mrk,mdk->mrd", factor_sq, basis_sq, precision=highest)
    delta_up = start_up - trained_up[0] + resid_up[0]
    factor_up = jnp.dot(delta_up, basis_up, precision=highest, preferred_element_type=jnp.float32)
    new_resid_up = delta_up - jnp.einsum("rk,fk->rf", factor_up, basis_up, precision=highest)
    delta_down = start_down - trained_down[0] + resid_down[0]
    factor_down = jnp.dot(
        delta_down, basis_down, precision=highest, preferred_element_type=jnp.float32
    )
    new_resid_down = delta_down - jnp.einsum(
        "rk,dk->rd", factor_down, basis_down, precision=highest
    )
    norm_delta = start_ln - trained_ln[0]
    summed = rep_sum((factor_sq, factor_up, factor_down, norm_delta))
    mean_sq = summed[0] / groups
    mean_up = summed[1] / groups
    mean_down = summed[2] / groups
    mean_ln = summed[3] / groups
    new_mom_ln, norm_weights = advance(start_ln, mom_ln, mean_ln)
    blocks_up = start_up.shape[1] // width
    blocks_down = start_down.shape[0] // rows
    start_all = jnp.concatenate(
        [start_sq, split_cols(start_up, width), start_down.reshape(blocks_down, rows, width)]
    )
    mom_all = jnp.concatenate(
        [mom_sq, split_cols(mom_up, width), mom_down.reshape(blocks_down, rows, width)]
    )
    mean_all = jnp.concatenate(
        [
            mean_sq,
            jnp.broadcast_to(mean_up[None], (blocks_up, rows, rank)),
            mean_down.reshape(blocks_down, rows, rank),
        ]
    )
    basis_all = jnp.concatenate(
        [
            basis_sq,
            basis_up.reshape(blocks_up, width, rank),
            jnp.broadcast_to(basis_down[None], (blocks_down, width, rank)),
        ]
    )
    outer_all = jnp.einsum("brk,bdk->brd", mean_all, basis_all, precision=highest)
    new_mom_all, owned_all = advance(start_all, mom_all, outer_all)
    new_mom_sq = new_mom_all[:square]
    new_mom_up = join_cols(new_mom_all[square : square + blocks_up])
    new_mom_down = new_mom_all[square + blocks_up :].reshape(-1, width)
    gathered = lax.all_gather(owned_all, "shard", axis=1, tiled=True)
    weights_sq, weights_up, weights_down = unpack(gathered, rows)
    weights_ln = lax.all_gather(norm_weights, "shard", axis=1, tiled=True)
    return (
        new_resid_sq[None],
        new_resid_up[None],
        new_resid_down[None],
        new_mom_sq,
        new_mom_up,
        new_mom_down,
        new_mom_ln,
        weights_sq,
        weights_up,
        weights_down,
        weights_ln,
    )


def solution(mesh):
    placed = (
        P("rep", None, "shard", None),
        P("rep", "shard", None),
        P("rep", "shard", None),
        P("rep", None, "shard"),
        P(None, "shard", None),
        P("shard", None),
        P("shard", None),
        P(None, "shard"),
        P("rep", None, "shard", None),
        P("rep", "shard", None),
        P("rep", "shard", None),
        P(None, "shard", None),
        P("shard", None),
        P("shard", None),
        P(None, "shard"),
        P(),
        P(),
        P(),
    )
    return jax.shard_map(
        on_device,
        mesh=mesh,
        in_specs=placed,
        out_specs=(
            P("rep", None, "shard", None),
            P("rep", "shard", None),
            P("rep", "shard", None),
            P(None, "shard", None),
            P("shard", None),
            P("shard", None),
            P(None, "shard"),
            P(),
            P(),
            P(),
            P(),
        ),
        check_vma=False,
    )
```

```python
import functools

import jax
import jax.numpy as jnp
from jax import lax
from jax.experimental import pallas as pl
from jax.sharding import PartitionSpec as P

moment_coef = 0.9
outer_rate = 0.7


def advance(start, moment, outer):
    new_moment = moment_coef * moment + outer
    weights = (start - outer_rate * (outer + moment_coef * new_moment)).astype(jnp.bfloat16)
    return (new_moment, weights)


def split_cols(a, width):
    return a.reshape(a.shape[0], -1, width).transpose(1, 0, 2)


def join_cols(a):
    return a.transpose(1, 0, 2).reshape(a.shape[1], -1)


def unpack_kernel(rows, g_ref, sq_ref, up_ref, down_ref):
    blocks = g_ref.shape[1]
    sq_ref[...] = g_ref[0]
    up_ref[...] = jnp.concatenate([g_ref[1, k] for k in range(blocks)], axis=1)
    x = g_ref[2].astype(jnp.float32)
    per_step = g_ref.shape[2] // rows
    pieces = [x[q, h * rows : (h + 1) * rows] for h in range(per_step) for q in range(blocks)]
    down_ref[...] = jnp.concatenate(pieces, axis=0).astype(down_ref.dtype)


def unpack(gathered, rows):
    kinds_blocks, total, width = gathered.shape
    blocks = kinds_blocks // 3
    g = gathered.reshape(3, blocks, total, width)
    step = 8 * rows
    dt = gathered.dtype
    nbytes = 2 * gathered.size * dt.itemsize
    return pl.pallas_call(
        functools.partial(unpack_kernel, rows),
        grid=(total // step,),
        in_specs=[pl.BlockSpec((3, blocks, step, width), lambda j: (0, 0, j, 0))],
        out_specs=[
            pl.BlockSpec((blocks, step, width), lambda j: (0, j, 0)),
            pl.BlockSpec((step, blocks * width), lambda j: (j, 0)),
            pl.BlockSpec((blocks * step, width), lambda j: (j, 0)),
        ],
        out_shape=[
            jax.ShapeDtypeStruct((blocks, total, width), dt),
            jax.ShapeDtypeStruct((total, blocks * width), dt),
            jax.ShapeDtypeStruct((blocks * total, width), dt),
        ],
        cost_estimate=pl.CostEstimate(flops=0, transcendentals=0, bytes_accessed=nbytes),
    )(g)


def rep_sum(parts):
    n = lax.axis_size("rep")
    step = 1
    while step < n:
        other = lax.ppermute(parts, "rep", [(i, i ^ step) for i in range(n)])
        parts = jax.tree.map(jnp.add, parts, other)
        step *= 2
    return parts


def on_device(
    trained_sq,
    trained_up,
    trained_down,
    trained_ln,
    start_sq,
    start_up,
    start_down,
    start_ln,
    resid_sq,
    resid_up,
    resid_down,
    mom_sq,
    mom_up,
    mom_down,
    mom_ln,
    basis_sq,
    basis_up,
    basis_down,
):
    highest = lax.Precision.HIGHEST
    groups = lax.axis_size("rep")
    square, rows, width = start_sq.shape
    rank = basis_sq.shape[-1]
    delta_sq = start_sq - trained_sq[0] + resid_sq[0]
    factor_sq = jnp.einsum("mrd,mdk->mrk", delta_sq, basis_sq, precision=highest)
    new_resid_sq = delta_sq - jnp.einsum("mrk,mdk->mrd", factor_sq, basis_sq, precision=highest)
    delta_up = start_up - trained_up[0] + resid_up[0]
    factor_up = jnp.dot(delta_up, basis_up, precision=highest, preferred_element_type=jnp.float32)
    new_resid_up = delta_up - jnp.einsum("rk,fk->rf", factor_up, basis_up, precision=highest)
    delta_down = start_down - trained_down[0] + resid_down[0]
    factor_down = jnp.dot(
        delta_down, basis_down, precision=highest, preferred_element_type=jnp.float32
    )
    new_resid_down = delta_down - jnp.einsum(
        "rk,dk->rd", factor_down, basis_down, precision=highest
    )
    norm_delta = start_ln - trained_ln[0]
    norm_flat = norm_delta.reshape(-1)
    norm_rows = -(-norm_flat.shape[0] // rank)
    norm_pad = jnp.pad(norm_flat, (0, norm_rows * rank - norm_flat.shape[0]))
    parts = [factor_sq.reshape(-1, rank), factor_up, factor_down, norm_pad.reshape(norm_rows, rank)]
    summed = rep_sum(jnp.concatenate(parts)) / groups
    cuts = [p.shape[0] for p in parts]
    at = [sum(cuts[:i]) for i in range(len(cuts))]
    mean_sq = summed[at[0] : at[1]].reshape(factor_sq.shape)
    mean_up = summed[at[1] : at[2]]
    mean_down = summed[at[2] : at[3]]
    mean_ln = summed[at[3] :].reshape(-1)[: norm_flat.shape[0]].reshape(norm_delta.shape)
    new_mom_ln, norm_weights = advance(start_ln, mom_ln, mean_ln)
    blocks_up = start_up.shape[1] // width
    blocks_down = start_down.shape[0] // rows
    start_all = jnp.concatenate(
        [start_sq, split_cols(start_up, width), start_down.reshape(blocks_down, rows, width)]
    )
    mom_all = jnp.concatenate(
        [mom_sq, split_cols(mom_up, width), mom_down.reshape(blocks_down, rows, width)]
    )
    mean_all = jnp.concatenate(
        [
            mean_sq,
            jnp.broadcast_to(mean_up[None], (blocks_up, rows, rank)),
            mean_down.reshape(blocks_down, rows, rank),
        ]
    )
    basis_all = jnp.concatenate(
        [
            basis_sq,
            basis_up.reshape(blocks_up, width, rank),
            jnp.broadcast_to(basis_down[None], (blocks_down, width, rank)),
        ]
    )
    outer_all = jnp.einsum("brk,bdk->brd", mean_all, basis_all, precision=highest)
    new_mom_all, owned_all = advance(start_all, mom_all, outer_all)
    new_mom_sq = new_mom_all[:square]
    new_mom_up = join_cols(new_mom_all[square : square + blocks_up])
    new_mom_down = new_mom_all[square + blocks_up :].reshape(-1, width)
    owned_all, norm_weights = lax.optimization_barrier((owned_all, norm_weights))
    gathered = lax.all_gather(owned_all, "shard", axis=1, tiled=True)
    weights_sq, weights_up, weights_down = unpack(gathered, rows)
    weights_ln = lax.all_gather(norm_weights, "shard", axis=1, tiled=True)
    return (
        new_resid_sq[None],
        new_resid_up[None],
        new_resid_down[None],
        new_mom_sq,
        new_mom_up,
        new_mom_down,
        new_mom_ln,
        weights_sq,
        weights_up,
        weights_down,
        weights_ln,
    )


def solution(mesh):
    placed = (
        P("rep", None, "shard", None),
        P("rep", "shard", None),
        P("rep", "shard", None),
        P("rep", None, "shard"),
        P(None, "shard", None),
        P("shard", None),
        P("shard", None),
        P(None, "shard"),
        P("rep", None, "shard", None),
        P("rep", "shard", None),
        P("rep", "shard", None),
        P(None, "shard", None),
        P("shard", None),
        P("shard", None),
        P(None, "shard"),
        P(),
        P(),
        P(),
    )
    return jax.shard_map(
        on_device,
        mesh=mesh,
        in_specs=placed,
        out_specs=(
            P("rep", None, "shard", None),
            P("rep", "shard", None),
            P("rep", "shard", None),
            P(None, "shard", None),
            P("shard", None),
            P("shard", None),
            P(None, "shard"),
            P(),
            P(),
            P(),
            P(),
        ),
        check_vma=False,
    )
```

```python
import functools

import jax
import jax.numpy as jnp
from jax import lax
from jax.experimental import pallas as pl
from jax.sharding import PartitionSpec as P

moment_coef = 0.9
outer_rate = 0.7


def advance(start, moment, outer):
    new_moment = moment_coef * moment + outer
    weights = (start - outer_rate * (outer + moment_coef * new_moment)).astype(jnp.bfloat16)
    return (new_moment, weights)


def split_cols(a, width):
    return a.reshape(a.shape[0], -1, width).transpose(1, 0, 2)


def join_cols(a):
    return a.transpose(1, 0, 2).reshape(a.shape[1], -1)


def unpack_kernel(rows, g_ref, sq_ref, up_ref, down_ref):
    blocks = g_ref.shape[1]
    sq_ref[...] = g_ref[0]
    up_ref[...] = jnp.concatenate([g_ref[1, k] for k in range(blocks)], axis=1)
    x = g_ref[2].astype(jnp.float32)
    per_step = g_ref.shape[2] // rows
    pieces = [x[q, h * rows : (h + 1) * rows] for h in range(per_step) for q in range(blocks)]
    down_ref[...] = jnp.concatenate(pieces, axis=0).astype(down_ref.dtype)


def unpack(gathered, rows):
    kinds_blocks, total, width = gathered.shape
    blocks = kinds_blocks // 3
    g = gathered.reshape(3, blocks, total, width)
    step = 8 * rows
    dt = gathered.dtype
    nbytes = 2 * gathered.size * dt.itemsize
    return pl.pallas_call(
        functools.partial(unpack_kernel, rows),
        grid=(total // step,),
        in_specs=[pl.BlockSpec((3, blocks, step, width), lambda j: (0, 0, j, 0))],
        out_specs=[
            pl.BlockSpec((blocks, step, width), lambda j: (0, j, 0)),
            pl.BlockSpec((step, blocks * width), lambda j: (j, 0)),
            pl.BlockSpec((blocks * step, width), lambda j: (j, 0)),
        ],
        out_shape=[
            jax.ShapeDtypeStruct((blocks, total, width), dt),
            jax.ShapeDtypeStruct((total, blocks * width), dt),
            jax.ShapeDtypeStruct((blocks * total, width), dt),
        ],
        cost_estimate=pl.CostEstimate(flops=0, transcendentals=0, bytes_accessed=nbytes),
    )(g)


def rep_sum(parts):
    n = lax.axis_size("rep")
    me = lax.axis_index("rep")
    held = [parts] + [
        lax.ppermute(parts, "rep", [(i, (i + d) % n) for i in range(n)]) for d in range(1, n)
    ]
    stack = jnp.stack(held)
    by_index = [lax.dynamic_index_in_dim(stack, (me - k) % n, keepdims=False) for k in range(n)]
    while len(by_index) > 1:
        by_index = [a + b for a, b in zip(by_index[::2], by_index[1::2])]
    return by_index[0]


def on_device(
    trained_sq,
    trained_up,
    trained_down,
    trained_ln,
    start_sq,
    start_up,
    start_down,
    start_ln,
    resid_sq,
    resid_up,
    resid_down,
    mom_sq,
    mom_up,
    mom_down,
    mom_ln,
    basis_sq,
    basis_up,
    basis_down,
):
    highest = lax.Precision.HIGHEST
    groups = lax.axis_size("rep")
    square, rows, width = start_sq.shape
    rank = basis_sq.shape[-1]
    delta_sq = start_sq - trained_sq[0] + resid_sq[0]
    factor_sq = jnp.einsum("mrd,mdk->mrk", delta_sq, basis_sq, precision=highest)
    new_resid_sq = delta_sq - jnp.einsum("mrk,mdk->mrd", factor_sq, basis_sq, precision=highest)
    delta_up = start_up - trained_up[0] + resid_up[0]
    factor_up = jnp.dot(delta_up, basis_up, precision=highest, preferred_element_type=jnp.float32)
    new_resid_up = delta_up - jnp.einsum("rk,fk->rf", factor_up, basis_up, precision=highest)
    delta_down = start_down - trained_down[0] + resid_down[0]
    factor_down = jnp.dot(
        delta_down, basis_down, precision=highest, preferred_element_type=jnp.float32
    )
    new_resid_down = delta_down - jnp.einsum(
        "rk,dk->rd", factor_down, basis_down, precision=highest
    )
    norm_delta = start_ln - trained_ln[0]
    norm_flat = norm_delta.reshape(-1)
    norm_rows = -(-norm_flat.shape[0] // rank)
    norm_pad = jnp.pad(norm_flat, (0, norm_rows * rank - norm_flat.shape[0]))
    parts = [factor_sq.reshape(-1, rank), factor_up, factor_down, norm_pad.reshape(norm_rows, rank)]
    summed = rep_sum(jnp.concatenate(parts)) / groups
    cuts = [p.shape[0] for p in parts]
    at = [sum(cuts[:i]) for i in range(len(cuts))]
    mean_sq = summed[at[0] : at[1]].reshape(factor_sq.shape)
    mean_up = summed[at[1] : at[2]]
    mean_down = summed[at[2] : at[3]]
    mean_ln = summed[at[3] :].reshape(-1)[: norm_flat.shape[0]].reshape(norm_delta.shape)
    blocks_up = start_up.shape[1] // width
    blocks_down = start_down.shape[0] // rows
    start_all = jnp.concatenate(
        [start_sq, split_cols(start_up, width), start_down.reshape(blocks_down, rows, width)]
    )
    mom_all = jnp.concatenate(
        [mom_sq, split_cols(mom_up, width), mom_down.reshape(blocks_down, rows, width)]
    )
    mean_all = jnp.concatenate(
        [
            mean_sq,
            jnp.broadcast_to(mean_up[None], (blocks_up, rows, rank)),
            mean_down.reshape(blocks_down, rows, rank),
        ]
    )
    basis_all = jnp.concatenate(
        [
            basis_sq,
            basis_up.reshape(blocks_up, width, rank),
            jnp.broadcast_to(basis_down[None], (blocks_down, width, rank)),
        ]
    )
    outer_all = jnp.einsum("brk,bdk->brd", mean_all, basis_all, precision=highest)
    new_mom_all, owned_all = advance(start_all, mom_all, outer_all)
    new_mom_sq = new_mom_all[:square]
    new_mom_up = join_cols(new_mom_all[square : square + blocks_up])
    new_mom_down = new_mom_all[square + blocks_up :].reshape(-1, width)
    owned_all, mean_ln = lax.optimization_barrier((owned_all, mean_ln))
    new_mom_ln, norm_weights = advance(start_ln, mom_ln, mean_ln)
    gathered = lax.all_gather(owned_all, "shard", axis=1, tiled=True)
    weights_sq, weights_up, weights_down = unpack(gathered, rows)
    weights_ln = lax.all_gather(norm_weights, "shard", axis=1, tiled=True)
    return (
        new_resid_sq[None],
        new_resid_up[None],
        new_resid_down[None],
        new_mom_sq,
        new_mom_up,
        new_mom_down,
        new_mom_ln,
        weights_sq,
        weights_up,
        weights_down,
        weights_ln,
    )


def solution(mesh):
    placed = (
        P("rep", None, "shard", None),
        P("rep", "shard", None),
        P("rep", "shard", None),
        P("rep", None, "shard"),
        P(None, "shard", None),
        P("shard", None),
        P("shard", None),
        P(None, "shard"),
        P("rep", None, "shard", None),
        P("rep", "shard", None),
        P("rep", "shard", None),
        P(None, "shard", None),
        P("shard", None),
        P("shard", None),
        P(None, "shard"),
        P(),
        P(),
        P(),
    )
    return jax.shard_map(
        on_device,
        mesh=mesh,
        in_specs=placed,
        out_specs=(
            P("rep", None, "shard", None),
            P("rep", "shard", None),
            P("rep", "shard", None),
            P(None, "shard", None),
            P("shard", None),
            P("shard", None),
            P(None, "shard"),
            P(),
            P(),
            P(),
            P(),
        ),
        check_vma=False,
    )
```

```python
import functools

import jax
import jax.numpy as jnp
from jax import lax
from jax.experimental import pallas as pl
from jax.sharding import PartitionSpec as P

moment_coef = 0.9
outer_rate = 0.7


def advance(start, moment, outer):
    new_moment = moment_coef * moment + outer
    weights = (start - outer_rate * (outer + moment_coef * new_moment)).astype(jnp.bfloat16)
    return (new_moment, weights)


def split_cols(a, width):
    return a.reshape(a.shape[0], -1, width).transpose(1, 0, 2)


def join_cols(a):
    return a.transpose(1, 0, 2).reshape(a.shape[1], -1)


def unpack_kernel(rows, g_ref, sq_ref, up_ref, down_ref):
    blocks = g_ref.shape[1]
    sq_ref[...] = g_ref[0]
    up_ref[...] = jnp.concatenate([g_ref[1, k] for k in range(blocks)], axis=1)
    x = g_ref[2].astype(jnp.float32)
    per_step = g_ref.shape[2] // rows
    pieces = [x[q, h * rows : (h + 1) * rows] for h in range(per_step) for q in range(blocks)]
    down_ref[...] = jnp.concatenate(pieces, axis=0).astype(down_ref.dtype)


def unpack(gathered, rows):
    kinds_blocks, total, width = gathered.shape
    blocks = kinds_blocks // 3
    g = gathered.reshape(3, blocks, total, width)
    step = 8 * rows
    dt = gathered.dtype
    nbytes = 2 * gathered.size * dt.itemsize
    return pl.pallas_call(
        functools.partial(unpack_kernel, rows),
        grid=(total // step,),
        in_specs=[pl.BlockSpec((3, blocks, step, width), lambda j: (0, 0, j, 0))],
        out_specs=[
            pl.BlockSpec((blocks, step, width), lambda j: (0, j, 0)),
            pl.BlockSpec((step, blocks * width), lambda j: (j, 0)),
            pl.BlockSpec((blocks * step, width), lambda j: (j, 0)),
        ],
        out_shape=[
            jax.ShapeDtypeStruct((blocks, total, width), dt),
            jax.ShapeDtypeStruct((total, blocks * width), dt),
            jax.ShapeDtypeStruct((blocks * total, width), dt),
        ],
        cost_estimate=pl.CostEstimate(flops=0, transcendentals=0, bytes_accessed=nbytes),
    )(g)


def rep_sum(parts):
    n = lax.axis_size("rep")
    me = lax.axis_index("rep")
    held = [parts] + [
        lax.ppermute(parts, "rep", [(i, (i + d) % n) for i in range(n)]) for d in range(1, n)
    ]
    stack = jnp.stack(held)
    by_index = [lax.dynamic_index_in_dim(stack, (me - k) % n, keepdims=False) for k in range(n)]
    while len(by_index) > 1:
        by_index = [a + b for a, b in zip(by_index[::2], by_index[1::2])]
    return by_index[0]


def on_device(
    trained_sq,
    trained_up,
    trained_down,
    trained_ln,
    start_sq,
    start_up,
    start_down,
    start_ln,
    resid_sq,
    resid_up,
    resid_down,
    mom_sq,
    mom_up,
    mom_down,
    mom_ln,
    basis_sq,
    basis_up,
    basis_down,
):
    highest = lax.Precision.HIGHEST
    groups = lax.axis_size("rep")
    square, rows, width = start_sq.shape
    rank = basis_sq.shape[-1]
    delta_sq = start_sq - trained_sq[0] + resid_sq[0]
    factor_sq = jnp.einsum("mrd,mdk->mrk", delta_sq, basis_sq, precision=highest)
    new_resid_sq = delta_sq - jnp.einsum("mrk,mdk->mrd", factor_sq, basis_sq, precision=highest)
    delta_up = start_up - trained_up[0] + resid_up[0]
    factor_up = jnp.dot(delta_up, basis_up, precision=highest, preferred_element_type=jnp.float32)
    new_resid_up = delta_up - jnp.einsum("rk,fk->rf", factor_up, basis_up, precision=highest)
    delta_down = start_down - trained_down[0] + resid_down[0]
    factor_down = jnp.dot(
        delta_down, basis_down, precision=highest, preferred_element_type=jnp.float32
    )
    new_resid_down = delta_down - jnp.einsum(
        "rk,dk->rd", factor_down, basis_down, precision=highest
    )
    norm_delta = start_ln - trained_ln[0]
    blocks_up = start_up.shape[1] // width
    blocks_down = start_down.shape[0] // rows
    norm_cols = norm_delta.shape[0]
    norm_block = jnp.pad(norm_delta.T, ((0, 0), (0, rank - norm_cols)))
    stacked = jnp.concatenate(
        [
            factor_sq,
            jnp.broadcast_to(factor_up[None], (blocks_up, rows, rank)),
            factor_down.reshape(blocks_down, rows, rank),
            norm_block[None],
        ]
    )
    summed = rep_sum(stacked) / groups
    mean_all = summed[:-1]
    mean_ln = summed[-1, :, :norm_cols].T
    start_all = jnp.concatenate(
        [start_sq, split_cols(start_up, width), start_down.reshape(blocks_down, rows, width)]
    )
    mom_all = jnp.concatenate(
        [mom_sq, split_cols(mom_up, width), mom_down.reshape(blocks_down, rows, width)]
    )
    basis_all = jnp.concatenate(
        [
            basis_sq,
            basis_up.reshape(blocks_up, width, rank),
            jnp.broadcast_to(basis_down[None], (blocks_down, width, rank)),
        ]
    )
    outer_all = jnp.einsum("brk,bdk->brd", mean_all, basis_all, precision=highest)
    new_mom_all, owned_all = advance(start_all, mom_all, outer_all)
    new_mom_sq = new_mom_all[:square]
    new_mom_up = join_cols(new_mom_all[square : square + blocks_up])
    new_mom_down = new_mom_all[square + blocks_up :].reshape(-1, width)
    owned_all, mean_ln = lax.optimization_barrier((owned_all, mean_ln))
    new_mom_ln, norm_weights = advance(start_ln, mom_ln, mean_ln)
    gathered = lax.all_gather(owned_all, "shard", axis=1, tiled=True)
    weights_sq, weights_up, weights_down = unpack(gathered, rows)
    weights_ln = lax.all_gather(norm_weights, "shard", axis=1, tiled=True)
    return (
        new_resid_sq[None],
        new_resid_up[None],
        new_resid_down[None],
        new_mom_sq,
        new_mom_up,
        new_mom_down,
        new_mom_ln,
        weights_sq,
        weights_up,
        weights_down,
        weights_ln,
    )


def solution(mesh):
    placed = (
        P("rep", None, "shard", None),
        P("rep", "shard", None),
        P("rep", "shard", None),
        P("rep", None, "shard"),
        P(None, "shard", None),
        P("shard", None),
        P("shard", None),
        P(None, "shard"),
        P("rep", None, "shard", None),
        P("rep", "shard", None),
        P("rep", "shard", None),
        P(None, "shard", None),
        P("shard", None),
        P("shard", None),
        P(None, "shard"),
        P(),
        P(),
        P(),
    )
    return jax.shard_map(
        on_device,
        mesh=mesh,
        in_specs=placed,
        out_specs=(
            P("rep", None, "shard", None),
            P("rep", "shard", None),
            P("rep", "shard", None),
            P(None, "shard", None),
            P("shard", None),
            P("shard", None),
            P(None, "shard"),
            P(),
            P(),
            P(),
            P(),
        ),
        check_vma=False,
    )
```

```python
import functools

import jax
import jax.numpy as jnp
from jax import lax
from jax.experimental import pallas as pl
from jax.sharding import PartitionSpec as P

moment_coef = 0.9
outer_rate = 0.7


def advance(start, moment, outer):
    new_moment = moment_coef * moment + outer
    weights = (start - outer_rate * (outer + moment_coef * new_moment)).astype(jnp.bfloat16)
    return (new_moment, weights)


def split_cols(a, width):
    return a.reshape(a.shape[0], -1, width).transpose(1, 0, 2)


def join_cols(a):
    return a.transpose(1, 0, 2).reshape(a.shape[1], -1)


def unpack_kernel(rows, g_ref, sq_ref, up_ref, down_ref):
    blocks = g_ref.shape[1]
    sq_ref[...] = g_ref[0]
    up_ref[...] = jnp.concatenate([g_ref[1, k] for k in range(blocks)], axis=1)
    x = g_ref[2].astype(jnp.float32)
    per_step = g_ref.shape[2] // rows
    pieces = [x[q, h * rows : (h + 1) * rows] for h in range(per_step) for q in range(blocks)]
    down_ref[...] = jnp.concatenate(pieces, axis=0).astype(down_ref.dtype)


def unpack(gathered, rows):
    kinds_blocks, total, width = gathered.shape
    blocks = kinds_blocks // 3
    g = gathered.reshape(3, blocks, total, width)
    step = 8 * rows
    dt = gathered.dtype
    nbytes = 2 * gathered.size * dt.itemsize
    return pl.pallas_call(
        functools.partial(unpack_kernel, rows),
        grid=(total // step,),
        in_specs=[pl.BlockSpec((3, blocks, step, width), lambda j: (0, 0, j, 0))],
        out_specs=[
            pl.BlockSpec((blocks, step, width), lambda j: (0, j, 0)),
            pl.BlockSpec((step, blocks * width), lambda j: (j, 0)),
            pl.BlockSpec((blocks * step, width), lambda j: (j, 0)),
        ],
        out_shape=[
            jax.ShapeDtypeStruct((blocks, total, width), dt),
            jax.ShapeDtypeStruct((total, blocks * width), dt),
            jax.ShapeDtypeStruct((blocks * total, width), dt),
        ],
        cost_estimate=pl.CostEstimate(flops=0, transcendentals=0, bytes_accessed=nbytes),
    )(g)


def rep_sum(parts):
    n = lax.axis_size("rep")
    me = lax.axis_index("rep")
    held = [parts] + [
        lax.ppermute(parts, "rep", [(i, (i + d) % n) for i in range(n)]) for d in range(1, n)
    ]
    stack = jnp.stack(held)
    by_index = [lax.dynamic_index_in_dim(stack, (me - k) % n, keepdims=False) for k in range(n)]
    while len(by_index) > 1:
        by_index = [a + b for a, b in zip(by_index[::2], by_index[1::2])]
    return by_index[0]


def on_device(
    trained_sq,
    trained_up,
    trained_down,
    trained_ln,
    start_sq,
    start_up,
    start_down,
    start_ln,
    resid_sq,
    resid_up,
    resid_down,
    mom_sq,
    mom_up,
    mom_down,
    mom_ln,
    basis_sq,
    basis_up,
    basis_down,
):
    highest = lax.Precision.HIGH
    groups = lax.axis_size("rep")
    square, rows, width = start_sq.shape
    rank = basis_sq.shape[-1]
    delta_sq = start_sq - trained_sq[0] + resid_sq[0]
    factor_sq = jnp.einsum("mrd,mdk->mrk", delta_sq, basis_sq, precision=highest)
    new_resid_sq = delta_sq - jnp.einsum("mrk,mdk->mrd", factor_sq, basis_sq, precision=highest)
    delta_up = start_up - trained_up[0] + resid_up[0]
    factor_up = jnp.dot(delta_up, basis_up, precision=highest, preferred_element_type=jnp.float32)
    new_resid_up = delta_up - jnp.einsum("rk,fk->rf", factor_up, basis_up, precision=highest)
    delta_down = start_down - trained_down[0] + resid_down[0]
    factor_down = jnp.dot(
        delta_down, basis_down, precision=highest, preferred_element_type=jnp.float32
    )
    new_resid_down = delta_down - jnp.einsum(
        "rk,dk->rd", factor_down, basis_down, precision=highest
    )
    norm_delta = start_ln - trained_ln[0]
    blocks_up = start_up.shape[1] // width
    blocks_down = start_down.shape[0] // rows
    norm_cols = norm_delta.shape[0]
    norm_block = jnp.pad(norm_delta.T, ((0, 0), (0, rank - norm_cols)))
    stacked = jnp.concatenate(
        [
            factor_sq,
            jnp.broadcast_to(factor_up[None], (blocks_up, rows, rank)),
            factor_down.reshape(blocks_down, rows, rank),
            norm_block[None],
        ]
    )
    summed = rep_sum(stacked) / groups
    mean_all = summed[:-1]
    mean_ln = summed[-1, :, :norm_cols].T
    start_all = jnp.concatenate(
        [start_sq, split_cols(start_up, width), start_down.reshape(blocks_down, rows, width)]
    )
    mom_all = jnp.concatenate(
        [mom_sq, split_cols(mom_up, width), mom_down.reshape(blocks_down, rows, width)]
    )
    basis_all = jnp.concatenate(
        [
            basis_sq,
            basis_up.reshape(blocks_up, width, rank),
            jnp.broadcast_to(basis_down[None], (blocks_down, width, rank)),
        ]
    )
    outer_all = jnp.einsum("brk,bdk->brd", mean_all, basis_all, precision=highest)
    new_mom_all, owned_all = advance(start_all, mom_all, outer_all)
    new_mom_sq = new_mom_all[:square]
    new_mom_up = join_cols(new_mom_all[square : square + blocks_up])
    new_mom_down = new_mom_all[square + blocks_up :].reshape(-1, width)
    owned_all, mean_ln = lax.optimization_barrier((owned_all, mean_ln))
    new_mom_ln, norm_weights = advance(start_ln, mom_ln, mean_ln)
    gathered = lax.all_gather(owned_all, "shard", axis=1, tiled=True)
    weights_sq, weights_up, weights_down = unpack(gathered, rows)
    weights_ln = lax.all_gather(norm_weights, "shard", axis=1, tiled=True)
    return (
        new_resid_sq[None],
        new_resid_up[None],
        new_resid_down[None],
        new_mom_sq,
        new_mom_up,
        new_mom_down,
        new_mom_ln,
        weights_sq,
        weights_up,
        weights_down,
        weights_ln,
    )


def solution(mesh):
    placed = (
        P("rep", None, "shard", None),
        P("rep", "shard", None),
        P("rep", "shard", None),
        P("rep", None, "shard"),
        P(None, "shard", None),
        P("shard", None),
        P("shard", None),
        P(None, "shard"),
        P("rep", None, "shard", None),
        P("rep", "shard", None),
        P("rep", "shard", None),
        P(None, "shard", None),
        P("shard", None),
        P("shard", None),
        P(None, "shard"),
        P(),
        P(),
        P(),
    )
    return jax.shard_map(
        on_device,
        mesh=mesh,
        in_specs=placed,
        out_specs=(
            P("rep", None, "shard", None),
            P("rep", "shard", None),
            P("rep", "shard", None),
            P(None, "shard", None),
            P("shard", None),
            P("shard", None),
            P(None, "shard"),
            P(),
            P(),
            P(),
            P(),
        ),
        check_vma=False,
    )
```

```python
import functools

import jax
import jax.numpy as jnp
from jax import lax
from jax.experimental import pallas as pl
from jax.sharding import PartitionSpec as P

moment_coef = 0.9
outer_rate = 0.7


def advance(start, moment, outer):
    new_moment = moment_coef * moment + outer
    weights = (start - outer_rate * (outer + moment_coef * new_moment)).astype(jnp.bfloat16)
    return (new_moment, weights)


def split_cols(a, width):
    return a.reshape(a.shape[0], -1, width).transpose(1, 0, 2)


def join_cols(a):
    return a.transpose(1, 0, 2).reshape(a.shape[1], -1)


def unpack_kernel(rows, g_ref, sq_ref, up_ref, down_ref):
    blocks = g_ref.shape[1]
    sq_ref[...] = g_ref[0]
    up_ref[...] = jnp.concatenate([g_ref[1, k] for k in range(blocks)], axis=1)
    x = g_ref[2].astype(jnp.float32)
    per_step = g_ref.shape[2] // rows
    pieces = [x[q, h * rows : (h + 1) * rows] for h in range(per_step) for q in range(blocks)]
    down_ref[...] = jnp.concatenate(pieces, axis=0).astype(down_ref.dtype)


def unpack(gathered, rows):
    kinds_blocks, total, width = gathered.shape
    blocks = kinds_blocks // 3
    g = gathered.reshape(3, blocks, total, width)
    step = 8 * rows
    dt = gathered.dtype
    nbytes = 2 * gathered.size * dt.itemsize
    return pl.pallas_call(
        functools.partial(unpack_kernel, rows),
        grid=(total // step,),
        in_specs=[pl.BlockSpec((3, blocks, step, width), lambda j: (0, 0, j, 0))],
        out_specs=[
            pl.BlockSpec((blocks, step, width), lambda j: (0, j, 0)),
            pl.BlockSpec((step, blocks * width), lambda j: (j, 0)),
            pl.BlockSpec((blocks * step, width), lambda j: (j, 0)),
        ],
        out_shape=[
            jax.ShapeDtypeStruct((blocks, total, width), dt),
            jax.ShapeDtypeStruct((total, blocks * width), dt),
            jax.ShapeDtypeStruct((blocks * total, width), dt),
        ],
        cost_estimate=pl.CostEstimate(flops=0, transcendentals=0, bytes_accessed=nbytes),
    )(g)


def rep_sum(parts):
    n = lax.axis_size("rep")
    me = lax.axis_index("rep")
    held = [parts] + [
        lax.ppermute(parts, "rep", [(i, (i + d) % n) for i in range(n)]) for d in range(1, n)
    ]
    stack = jnp.stack(held)
    by_index = [lax.dynamic_index_in_dim(stack, (me - k) % n, keepdims=False) for k in range(n)]
    while len(by_index) > 1:
        by_index = [a + b for a, b in zip(by_index[::2], by_index[1::2])]
    return by_index[0]


def on_device(
    trained_sq,
    trained_up,
    trained_down,
    trained_ln,
    start_sq,
    start_up,
    start_down,
    start_ln,
    resid_sq,
    resid_up,
    resid_down,
    mom_sq,
    mom_up,
    mom_down,
    mom_ln,
    basis_sq,
    basis_up,
    basis_down,
):
    highest = lax.Precision.HIGHEST
    groups = lax.axis_size("rep")
    square, rows, width = start_sq.shape
    rank = basis_sq.shape[-1]
    delta_sq = start_sq - trained_sq[0] + resid_sq[0]
    factor_sq = jnp.einsum("mrd,mdk->mrk", delta_sq, basis_sq, precision=highest)
    new_resid_sq = delta_sq - jnp.einsum("mrk,mdk->mrd", factor_sq, basis_sq, precision=highest)
    delta_up = start_up - trained_up[0] + resid_up[0]
    blocks_up = start_up.shape[1] // width
    basis_up_blocks = basis_up.reshape(blocks_up, width, rank)
    factor_up = jnp.einsum(
        "krd,kdc->krc", split_cols(delta_up, width), basis_up_blocks, precision=highest
    ).sum(0)
    new_resid_up = delta_up - jnp.einsum("rk,fk->rf", factor_up, basis_up, precision=highest)
    delta_down = start_down - trained_down[0] + resid_down[0]
    blocks_down = start_down.shape[0] // rows
    factor_down = jnp.einsum(
        "qrd,dc->qrc", delta_down.reshape(blocks_down, rows, width), basis_down, precision=highest
    ).reshape(-1, rank)
    new_resid_down = delta_down - jnp.einsum(
        "rk,dk->rd", factor_down, basis_down, precision=highest
    )
    norm_delta = start_ln - trained_ln[0]
    norm_cols = norm_delta.shape[0]
    norm_block = jnp.pad(norm_delta.T, ((0, 0), (0, rank - norm_cols)))
    stacked = jnp.concatenate(
        [
            factor_sq,
            jnp.broadcast_to(factor_up[None], (blocks_up, rows, rank)),
            factor_down.reshape(blocks_down, rows, rank),
            norm_block[None],
        ]
    )
    summed = rep_sum(stacked) / groups
    mean_all = summed[:-1]
    mean_ln = summed[-1, :, :norm_cols].T
    start_all = jnp.concatenate(
        [start_sq, split_cols(start_up, width), start_down.reshape(blocks_down, rows, width)]
    )
    mom_all = jnp.concatenate(
        [mom_sq, split_cols(mom_up, width), mom_down.reshape(blocks_down, rows, width)]
    )
    basis_all = jnp.concatenate(
        [
            basis_sq,
            basis_up.reshape(blocks_up, width, rank),
            jnp.broadcast_to(basis_down[None], (blocks_down, width, rank)),
        ]
    )
    outer_all = jnp.einsum("brk,bdk->brd", mean_all, basis_all, precision=highest)
    new_mom_all, owned_all = advance(start_all, mom_all, outer_all)
    new_mom_sq = new_mom_all[:square]
    new_mom_up = join_cols(new_mom_all[square : square + blocks_up])
    new_mom_down = new_mom_all[square + blocks_up :].reshape(-1, width)
    owned_all, mean_ln = lax.optimization_barrier((owned_all, mean_ln))
    new_mom_ln, norm_weights = advance(start_ln, mom_ln, mean_ln)
    gathered = lax.all_gather(owned_all, "shard", axis=1, tiled=True)
    weights_sq, weights_up, weights_down = unpack(gathered, rows)
    weights_ln = lax.all_gather(norm_weights, "shard", axis=1, tiled=True)
    return (
        new_resid_sq[None],
        new_resid_up[None],
        new_resid_down[None],
        new_mom_sq,
        new_mom_up,
        new_mom_down,
        new_mom_ln,
        weights_sq,
        weights_up,
        weights_down,
        weights_ln,
    )


def solution(mesh):
    placed = (
        P("rep", None, "shard", None),
        P("rep", "shard", None),
        P("rep", "shard", None),
        P("rep", None, "shard"),
        P(None, "shard", None),
        P("shard", None),
        P("shard", None),
        P(None, "shard"),
        P("rep", None, "shard", None),
        P("rep", "shard", None),
        P("rep", "shard", None),
        P(None, "shard", None),
        P("shard", None),
        P("shard", None),
        P(None, "shard"),
        P(),
        P(),
        P(),
    )
    return jax.shard_map(
        on_device,
        mesh=mesh,
        in_specs=placed,
        out_specs=(
            P("rep", None, "shard", None),
            P("rep", "shard", None),
            P("rep", "shard", None),
            P(None, "shard", None),
            P("shard", None),
            P("shard", None),
            P(None, "shard"),
            P(),
            P(),
            P(),
            P(),
        ),
        check_vma=False,
    )
```

```python
import functools

import jax
import jax.numpy as jnp
from jax import lax
from jax.experimental import pallas as pl
from jax.sharding import PartitionSpec as P

moment_coef = 0.9
outer_rate = 0.7


def advance(start, moment, outer):
    new_moment = moment_coef * moment + outer
    weights = (start - outer_rate * (outer + moment_coef * new_moment)).astype(jnp.bfloat16)
    return (new_moment, weights)


def split_cols(a, width):
    return a.reshape(a.shape[0], -1, width).transpose(1, 0, 2)


def join_cols(a):
    return a.transpose(1, 0, 2).reshape(a.shape[1], -1)


def unpack_kernel(rows, g_ref, sq_ref, up_ref, down_ref):
    blocks = g_ref.shape[1]
    sq_ref[...] = g_ref[0]
    up_ref[...] = jnp.concatenate([g_ref[1, k] for k in range(blocks)], axis=1)
    x = g_ref[2].astype(jnp.float32)
    per_step = g_ref.shape[2] // rows
    pieces = [x[q, h * rows : (h + 1) * rows] for h in range(per_step) for q in range(blocks)]
    down_ref[...] = jnp.concatenate(pieces, axis=0).astype(down_ref.dtype)


def unpack(gathered, rows):
    kinds_blocks, total, width = gathered.shape
    blocks = kinds_blocks // 3
    g = gathered.reshape(3, blocks, total, width)
    step = 8 * rows
    dt = gathered.dtype
    nbytes = 2 * gathered.size * dt.itemsize
    return pl.pallas_call(
        functools.partial(unpack_kernel, rows),
        grid=(total // step,),
        in_specs=[pl.BlockSpec((3, blocks, step, width), lambda j: (0, 0, j, 0))],
        out_specs=[
            pl.BlockSpec((blocks, step, width), lambda j: (0, j, 0)),
            pl.BlockSpec((step, blocks * width), lambda j: (j, 0)),
            pl.BlockSpec((blocks * step, width), lambda j: (j, 0)),
        ],
        out_shape=[
            jax.ShapeDtypeStruct((blocks, total, width), dt),
            jax.ShapeDtypeStruct((total, blocks * width), dt),
            jax.ShapeDtypeStruct((blocks * total, width), dt),
        ],
        cost_estimate=pl.CostEstimate(flops=0, transcendentals=0, bytes_accessed=nbytes),
    )(g)


def factor_kernel(t_sq, s_sq, r_sq, b_sq, t_up, s_up, r_up, b_up, t_dn, s_dn, r_dn, b_dn, out):
    highest = lax.Precision.HIGHEST
    square, rows = s_sq.shape[0], s_sq.shape[1]
    for m in range(square):
        delta = s_sq[m] - t_sq[0, m] + r_sq[0, m]
        out[m] = jnp.dot(delta, b_sq[m], precision=highest, preferred_element_type=jnp.float32)
    delta = s_up[...] - t_up[0] + r_up[0]
    up = jnp.dot(delta, b_up[...], precision=highest, preferred_element_type=jnp.float32)
    blocks = (out.shape[0] - square) // 2
    for k in range(blocks):
        out[square + k] = up
    delta = s_dn[...] - t_dn[0] + r_dn[0]
    down = jnp.dot(delta, b_dn[...], precision=highest, preferred_element_type=jnp.float32)
    for q in range(blocks):
        out[square + blocks + q] = down[q * rows : (q + 1) * rows]


def factors(*operands):
    s_sq, b_sq, b_up, s_dn = operands[1], operands[3], operands[7], operands[9]
    square, rows, _ = s_sq.shape
    blocks = s_dn.shape[0] // rows
    rank = b_sq.shape[-1]
    nbytes = sum(o.size * o.dtype.itemsize for o in operands)
    flops = 2 * rank * sum(o.size for o in operands[1:12:4])
    return pl.pallas_call(
        factor_kernel,
        out_shape=jax.ShapeDtypeStruct((square + 2 * blocks, rows, rank), jnp.float32),
        cost_estimate=pl.CostEstimate(flops=flops, transcendentals=0, bytes_accessed=nbytes),
    )(*operands)


def rep_sum(parts):
    n = lax.axis_size("rep")
    me = lax.axis_index("rep")
    held = [parts] + [
        lax.ppermute(parts, "rep", [(i, (i + d) % n) for i in range(n)]) for d in range(1, n)
    ]
    stack = jnp.stack(held)
    by_index = [lax.dynamic_index_in_dim(stack, (me - k) % n, keepdims=False) for k in range(n)]
    while len(by_index) > 1:
        by_index = [a + b for a, b in zip(by_index[::2], by_index[1::2])]
    return by_index[0]


def on_device(
    trained_sq,
    trained_up,
    trained_down,
    trained_ln,
    start_sq,
    start_up,
    start_down,
    start_ln,
    resid_sq,
    resid_up,
    resid_down,
    mom_sq,
    mom_up,
    mom_down,
    mom_ln,
    basis_sq,
    basis_up,
    basis_down,
):
    highest = lax.Precision.HIGHEST
    groups = lax.axis_size("rep")
    square, rows, width = start_sq.shape
    rank = basis_sq.shape[-1]
    stack = factors(
        trained_sq, start_sq, resid_sq, basis_sq,
        trained_up, start_up, resid_up, basis_up,
        trained_down, start_down, resid_down, basis_down,
    )
    blocks_up = start_up.shape[1] // width
    blocks_down = start_down.shape[0] // rows
    factor_sq = stack[:square]
    factor_up = stack[square]
    factor_down = stack[square + blocks_up :].reshape(-1, rank)
    delta_sq = start_sq - trained_sq[0] + resid_sq[0]
    new_resid_sq = delta_sq - jnp.einsum("mrk,mdk->mrd", factor_sq, basis_sq, precision=highest)
    delta_up = start_up - trained_up[0] + resid_up[0]
    new_resid_up = delta_up - jnp.einsum("rk,fk->rf", factor_up, basis_up, precision=highest)
    delta_down = start_down - trained_down[0] + resid_down[0]
    new_resid_down = delta_down - jnp.einsum(
        "rk,dk->rd", factor_down, basis_down, precision=highest
    )
    norm_delta = start_ln - trained_ln[0]
    norm_cols = norm_delta.shape[0]
    norm_block = jnp.pad(norm_delta.T, ((0, 0), (0, rank - norm_cols)))
    stacked = jnp.concatenate([stack, norm_block[None]])
    summed = rep_sum(stacked) / groups
    mean_all = summed[:-1]
    mean_ln = summed[-1, :, :norm_cols].T
    start_all = jnp.concatenate(
        [start_sq, split_cols(start_up, width), start_down.reshape(blocks_down, rows, width)]
    )
    mom_all = jnp.concatenate(
        [mom_sq, split_cols(mom_up, width), mom_down.reshape(blocks_down, rows, width)]
    )
    basis_all = jnp.concatenate(
        [
            basis_sq,
            basis_up.reshape(blocks_up, width, rank),
            jnp.broadcast_to(basis_down[None], (blocks_down, width, rank)),
        ]
    )
    outer_all = jnp.einsum("brk,bdk->brd", mean_all, basis_all, precision=highest)
    new_mom_all, owned_all = advance(start_all, mom_all, outer_all)
    new_mom_sq = new_mom_all[:square]
    new_mom_up = join_cols(new_mom_all[square : square + blocks_up])
    new_mom_down = new_mom_all[square + blocks_up :].reshape(-1, width)
    owned_all, mean_ln = lax.optimization_barrier((owned_all, mean_ln))
    new_mom_ln, norm_weights = advance(start_ln, mom_ln, mean_ln)
    gathered = lax.all_gather(owned_all, "shard", axis=1, tiled=True)
    weights_sq, weights_up, weights_down = unpack(gathered, rows)
    weights_ln = lax.all_gather(norm_weights, "shard", axis=1, tiled=True)
    return (
        new_resid_sq[None],
        new_resid_up[None],
        new_resid_down[None],
        new_mom_sq,
        new_mom_up,
        new_mom_down,
        new_mom_ln,
        weights_sq,
        weights_up,
        weights_down,
        weights_ln,
    )


def solution(mesh):
    placed = (
        P("rep", None, "shard", None),
        P("rep", "shard", None),
        P("rep", "shard", None),
        P("rep", None, "shard"),
        P(None, "shard", None),
        P("shard", None),
        P("shard", None),
        P(None, "shard"),
        P("rep", None, "shard", None),
        P("rep", "shard", None),
        P("rep", "shard", None),
        P(None, "shard", None),
        P("shard", None),
        P("shard", None),
        P(None, "shard"),
        P(),
        P(),
        P(),
    )
    return jax.shard_map(
        on_device,
        mesh=mesh,
        in_specs=placed,
        out_specs=(
            P("rep", None, "shard", None),
            P("rep", "shard", None),
            P("rep", "shard", None),
            P(None, "shard", None),
            P("shard", None),
            P("shard", None),
            P(None, "shard"),
            P(),
            P(),
            P(),
            P(),
        ),
        check_vma=False,
    )
```

```python
import functools

import jax
import jax.numpy as jnp
from jax import lax
from jax.experimental import pallas as pl
from jax.sharding import PartitionSpec as P

moment_coef = 0.9
outer_rate = 0.7


def advance(start, moment, outer):
    new_moment = moment_coef * moment + outer
    weights = (start - outer_rate * (outer + moment_coef * new_moment)).astype(jnp.bfloat16)
    return (new_moment, weights)


def split_cols(a, width):
    return a.reshape(a.shape[0], -1, width).transpose(1, 0, 2)


def join_cols(a):
    return a.transpose(1, 0, 2).reshape(a.shape[1], -1)


def unpack_kernel(rows, g_ref, sq_ref, up_ref, down_ref):
    blocks = g_ref.shape[1]
    sq_ref[...] = g_ref[0]
    up_ref[...] = jnp.concatenate([g_ref[1, k] for k in range(blocks)], axis=1)
    x = g_ref[2].astype(jnp.float32)
    per_step = g_ref.shape[2] // rows
    pieces = [x[q, h * rows : (h + 1) * rows] for h in range(per_step) for q in range(blocks)]
    down_ref[...] = jnp.concatenate(pieces, axis=0).astype(down_ref.dtype)


def unpack(gathered, rows):
    kinds_blocks, total, width = gathered.shape
    blocks = kinds_blocks // 3
    g = gathered.reshape(3, blocks, total, width)
    step = 8 * rows
    dt = gathered.dtype
    nbytes = 2 * gathered.size * dt.itemsize
    return pl.pallas_call(
        functools.partial(unpack_kernel, rows),
        grid=(total // step,),
        in_specs=[pl.BlockSpec((3, blocks, step, width), lambda j: (0, 0, j, 0))],
        out_specs=[
            pl.BlockSpec((blocks, step, width), lambda j: (0, j, 0)),
            pl.BlockSpec((step, blocks * width), lambda j: (j, 0)),
            pl.BlockSpec((blocks * step, width), lambda j: (j, 0)),
        ],
        out_shape=[
            jax.ShapeDtypeStruct((blocks, total, width), dt),
            jax.ShapeDtypeStruct((total, blocks * width), dt),
            jax.ShapeDtypeStruct((blocks * total, width), dt),
        ],
        cost_estimate=pl.CostEstimate(flops=0, transcendentals=0, bytes_accessed=nbytes),
    )(g)


def rep_sum(parts):
    n = lax.axis_size("rep")
    me = lax.axis_index("rep")
    held = [parts] + [
        lax.ppermute(parts, "rep", [(i, (i + d) % n) for i in range(n)]) for d in range(1, n)
    ]
    stack = jnp.stack(held)
    by_index = [lax.dynamic_index_in_dim(stack, (me - k) % n, keepdims=False) for k in range(n)]
    while len(by_index) > 1:
        by_index = [a + b for a, b in zip(by_index[::2], by_index[1::2])]
    return by_index[0]


def on_device(
    trained_sq,
    trained_up,
    trained_down,
    trained_ln,
    start_sq,
    start_up,
    start_down,
    start_ln,
    resid_sq,
    resid_up,
    resid_down,
    mom_sq,
    mom_up,
    mom_down,
    mom_ln,
    basis_sq,
    basis_up,
    basis_down,
):
    highest = lax.Precision.HIGHEST
    groups = lax.axis_size("rep")
    square, rows, width = start_sq.shape
    rank = basis_sq.shape[-1]
    delta_sq = start_sq - trained_sq[0] + resid_sq[0]
    factor_sq = jnp.einsum("mrd,mdk->mrk", delta_sq, basis_sq, precision=highest)
    new_resid_sq = delta_sq - jnp.einsum("mrk,mdk->mrd", factor_sq, basis_sq, precision=highest)
    delta_up = start_up - trained_up[0] + resid_up[0]
    factor_up = jnp.dot(delta_up, basis_up, precision=highest, preferred_element_type=jnp.float32)
    new_resid_up = delta_up - jnp.einsum("rk,fk->rf", factor_up, basis_up, precision=highest)
    delta_down = start_down - trained_down[0] + resid_down[0]
    factor_down = jnp.dot(
        delta_down, basis_down, precision=highest, preferred_element_type=jnp.float32
    )
    new_resid_down = delta_down - jnp.einsum(
        "rk,dk->rd", factor_down, basis_down, precision=highest
    )
    norm_delta = start_ln - trained_ln[0]
    norm_flat = norm_delta.reshape(-1)
    norm_rows = -(-norm_flat.shape[0] // rank)
    norm_pad = jnp.pad(norm_flat, (0, norm_rows * rank - norm_flat.shape[0]))
    parts = [factor_sq.reshape(-1, rank), factor_up, factor_down, norm_pad.reshape(norm_rows, rank)]
    summed = rep_sum(jnp.concatenate(parts)) / groups
    cuts = [p.shape[0] for p in parts]
    at = [sum(cuts[:i]) for i in range(len(cuts))]
    mean_sq = summed[at[0] : at[1]].reshape(factor_sq.shape)
    mean_up = summed[at[1] : at[2]]
    mean_down = summed[at[2] : at[3]]
    mean_ln = summed[at[3] :].reshape(-1)[: norm_flat.shape[0]].reshape(norm_delta.shape)
    blocks_up = start_up.shape[1] // width
    blocks_down = start_down.shape[0] // rows
    start_all = jnp.concatenate(
        [start_sq, split_cols(start_up, width), start_down.reshape(blocks_down, rows, width)]
    )
    mom_all = jnp.concatenate(
        [mom_sq, split_cols(mom_up, width), mom_down.reshape(blocks_down, rows, width)]
    )
    mean_all = jnp.concatenate(
        [
            mean_sq,
            jnp.broadcast_to(mean_up[None], (blocks_up, rows, rank)),
            mean_down.reshape(blocks_down, rows, rank),
        ]
    )
    basis_all = jnp.concatenate(
        [
            basis_sq,
            basis_up.reshape(blocks_up, width, rank),
            jnp.broadcast_to(basis_down[None], (blocks_down, width, rank)),
        ]
    )
    outer_all = jnp.einsum(
        "brk,bdk->brd", mean_all, basis_all, precision=lax.Precision.HIGH
    )
    new_mom_all, owned_all = advance(start_all, mom_all, outer_all)
    new_mom_sq = new_mom_all[:square]
    new_mom_up = join_cols(new_mom_all[square : square + blocks_up])
    new_mom_down = new_mom_all[square + blocks_up :].reshape(-1, width)
    owned_all, mean_ln = lax.optimization_barrier((owned_all, mean_ln))
    new_mom_ln, norm_weights = advance(start_ln, mom_ln, mean_ln)
    gathered = lax.all_gather(owned_all, "shard", axis=1, tiled=True)
    weights_sq, weights_up, weights_down = unpack(gathered, rows)
    weights_ln = lax.all_gather(norm_weights, "shard", axis=1, tiled=True)
    return (
        new_resid_sq[None],
        new_resid_up[None],
        new_resid_down[None],
        new_mom_sq,
        new_mom_up,
        new_mom_down,
        new_mom_ln,
        weights_sq,
        weights_up,
        weights_down,
        weights_ln,
    )


def solution(mesh):
    placed = (
        P("rep", None, "shard", None),
        P("rep", "shard", None),
        P("rep", "shard", None),
        P("rep", None, "shard"),
        P(None, "shard", None),
        P("shard", None),
        P("shard", None),
        P(None, "shard"),
        P("rep", None, "shard", None),
        P("rep", "shard", None),
        P("rep", "shard", None),
        P(None, "shard", None),
        P("shard", None),
        P("shard", None),
        P(None, "shard"),
        P(),
        P(),
        P(),
    )
    return jax.shard_map(
        on_device,
        mesh=mesh,
        in_specs=placed,
        out_specs=(
            P("rep", None, "shard", None),
            P("rep", "shard", None),
            P("rep", "shard", None),
            P(None, "shard", None),
            P("shard", None),
            P("shard", None),
            P(None, "shard"),
            P(),
            P(),
            P(),
            P(),
        ),
        check_vma=False,
    )
```

```python
import functools

import jax
import jax.numpy as jnp
from jax import lax
from jax.experimental import pallas as pl
from jax.sharding import PartitionSpec as P

moment_coef = 0.9
outer_rate = 0.7


def advance(start, moment, outer):
    new_moment = moment_coef * moment + outer
    weights = (start - outer_rate * (outer + moment_coef * new_moment)).astype(jnp.bfloat16)
    return (new_moment, weights)


def split_cols(a, width):
    return a.reshape(a.shape[0], -1, width).transpose(1, 0, 2)


def join_cols(a):
    return a.transpose(1, 0, 2).reshape(a.shape[1], -1)


def unpack_kernel(rows, g_ref, sq_ref, up_ref, down_ref):
    blocks = g_ref.shape[1]
    sq_ref[...] = g_ref[0]
    up_ref[...] = jnp.concatenate([g_ref[1, k] for k in range(blocks)], axis=1)
    x = g_ref[2].astype(jnp.float32)
    per_step = g_ref.shape[2] // rows
    pieces = [x[q, h * rows : (h + 1) * rows] for h in range(per_step) for q in range(blocks)]
    down_ref[...] = jnp.concatenate(pieces, axis=0).astype(down_ref.dtype)


def unpack(gathered, rows):
    kinds_blocks, total, width = gathered.shape
    blocks = kinds_blocks // 3
    g = gathered.reshape(3, blocks, total, width)
    step = 8 * rows
    dt = gathered.dtype
    nbytes = 2 * gathered.size * dt.itemsize
    return pl.pallas_call(
        functools.partial(unpack_kernel, rows),
        grid=(total // step,),
        in_specs=[pl.BlockSpec((3, blocks, step, width), lambda j: (0, 0, j, 0))],
        out_specs=[
            pl.BlockSpec((blocks, step, width), lambda j: (0, j, 0)),
            pl.BlockSpec((step, blocks * width), lambda j: (j, 0)),
            pl.BlockSpec((blocks * step, width), lambda j: (j, 0)),
        ],
        out_shape=[
            jax.ShapeDtypeStruct((blocks, total, width), dt),
            jax.ShapeDtypeStruct((total, blocks * width), dt),
            jax.ShapeDtypeStruct((blocks * total, width), dt),
        ],
        cost_estimate=pl.CostEstimate(flops=0, transcendentals=0, bytes_accessed=nbytes),
    )(g)


def rep_sum(parts):
    n = lax.axis_size("rep")
    copies = jnp.broadcast_to(parts[None], (n,) + parts.shape)
    held = lax.all_to_all(copies, "rep", 0, 0, tiled=True)
    by_index = [held[k] for k in range(n)]
    while len(by_index) > 1:
        by_index = [a + b for a, b in zip(by_index[::2], by_index[1::2])]
    return by_index[0]


def on_device(
    trained_sq,
    trained_up,
    trained_down,
    trained_ln,
    start_sq,
    start_up,
    start_down,
    start_ln,
    resid_sq,
    resid_up,
    resid_down,
    mom_sq,
    mom_up,
    mom_down,
    mom_ln,
    basis_sq,
    basis_up,
    basis_down,
):
    highest = lax.Precision.HIGHEST
    groups = lax.axis_size("rep")
    square, rows, width = start_sq.shape
    rank = basis_sq.shape[-1]
    delta_sq = start_sq - trained_sq[0] + resid_sq[0]
    factor_sq = jnp.einsum("mrd,mdk->mrk", delta_sq, basis_sq, precision=highest)
    new_resid_sq = delta_sq - jnp.einsum("mrk,mdk->mrd", factor_sq, basis_sq, precision=highest)
    delta_up = start_up - trained_up[0] + resid_up[0]
    factor_up = jnp.dot(delta_up, basis_up, precision=highest, preferred_element_type=jnp.float32)
    new_resid_up = delta_up - jnp.einsum("rk,fk->rf", factor_up, basis_up, precision=highest)
    delta_down = start_down - trained_down[0] + resid_down[0]
    factor_down = jnp.dot(
        delta_down, basis_down, precision=highest, preferred_element_type=jnp.float32
    )
    new_resid_down = delta_down - jnp.einsum(
        "rk,dk->rd", factor_down, basis_down, precision=highest
    )
    norm_delta = start_ln - trained_ln[0]
    norm_flat = norm_delta.reshape(-1)
    norm_rows = -(-norm_flat.shape[0] // rank)
    norm_pad = jnp.pad(norm_flat, (0, norm_rows * rank - norm_flat.shape[0]))
    parts = [factor_sq.reshape(-1, rank), factor_up, factor_down, norm_pad.reshape(norm_rows, rank)]
    summed = rep_sum(jnp.concatenate(parts)) / groups
    cuts = [p.shape[0] for p in parts]
    at = [sum(cuts[:i]) for i in range(len(cuts))]
    mean_sq = summed[at[0] : at[1]].reshape(factor_sq.shape)
    mean_up = summed[at[1] : at[2]]
    mean_down = summed[at[2] : at[3]]
    mean_ln = summed[at[3] :].reshape(-1)[: norm_flat.shape[0]].reshape(norm_delta.shape)
    blocks_up = start_up.shape[1] // width
    blocks_down = start_down.shape[0] // rows
    start_all = jnp.concatenate(
        [start_sq, split_cols(start_up, width), start_down.reshape(blocks_down, rows, width)]
    )
    mom_all = jnp.concatenate(
        [mom_sq, split_cols(mom_up, width), mom_down.reshape(blocks_down, rows, width)]
    )
    mean_all = jnp.concatenate(
        [
            mean_sq,
            jnp.broadcast_to(mean_up[None], (blocks_up, rows, rank)),
            mean_down.reshape(blocks_down, rows, rank),
        ]
    )
    basis_all = jnp.concatenate(
        [
            basis_sq,
            basis_up.reshape(blocks_up, width, rank),
            jnp.broadcast_to(basis_down[None], (blocks_down, width, rank)),
        ]
    )
    outer_all = jnp.einsum("brk,bdk->brd", mean_all, basis_all, precision=highest)
    new_mom_all, owned_all = advance(start_all, mom_all, outer_all)
    new_mom_sq = new_mom_all[:square]
    new_mom_up = join_cols(new_mom_all[square : square + blocks_up])
    new_mom_down = new_mom_all[square + blocks_up :].reshape(-1, width)
    owned_all, mean_ln = lax.optimization_barrier((owned_all, mean_ln))
    new_mom_ln, norm_weights = advance(start_ln, mom_ln, mean_ln)
    gathered = lax.all_gather(owned_all, "shard", axis=1, tiled=True)
    weights_sq, weights_up, weights_down = unpack(gathered, rows)
    weights_ln = lax.all_gather(norm_weights, "shard", axis=1, tiled=True)
    return (
        new_resid_sq[None],
        new_resid_up[None],
        new_resid_down[None],
        new_mom_sq,
        new_mom_up,
        new_mom_down,
        new_mom_ln,
        weights_sq,
        weights_up,
        weights_down,
        weights_ln,
    )


def solution(mesh):
    placed = (
        P("rep", None, "shard", None),
        P("rep", "shard", None),
        P("rep", "shard", None),
        P("rep", None, "shard"),
        P(None, "shard", None),
        P("shard", None),
        P("shard", None),
        P(None, "shard"),
        P("rep", None, "shard", None),
        P("rep", "shard", None),
        P("rep", "shard", None),
        P(None, "shard", None),
        P("shard", None),
        P("shard", None),
        P(None, "shard"),
        P(),
        P(),
        P(),
    )
    return jax.shard_map(
        on_device,
        mesh=mesh,
        in_specs=placed,
        out_specs=(
            P("rep", None, "shard", None),
            P("rep", "shard", None),
            P("rep", "shard", None),
            P(None, "shard", None),
            P("shard", None),
            P("shard", None),
            P(None, "shard"),
            P(),
            P(),
            P(),
            P(),
        ),
        check_vma=False,
    )
```

```python
import functools

import jax
import jax.numpy as jnp
from jax import lax
from jax.experimental import pallas as pl
from jax.sharding import PartitionSpec as P

moment_coef = 0.9
outer_rate = 0.7


def advance(start, moment, outer):
    new_moment = moment_coef * moment + outer
    weights = (start - outer_rate * (outer + moment_coef * new_moment)).astype(jnp.bfloat16)
    return (new_moment, weights)


def split_cols(a, width):
    return a.reshape(a.shape[0], -1, width).transpose(1, 0, 2)


def join_cols(a):
    return a.transpose(1, 0, 2).reshape(a.shape[1], -1)


def unpack_kernel(rows, g_ref, sq_ref, up_ref, down_ref):
    blocks = g_ref.shape[1]
    sq_ref[...] = g_ref[0]
    up_ref[...] = jnp.concatenate([g_ref[1, k] for k in range(blocks)], axis=1)
    x = g_ref[2].astype(jnp.float32)
    per_step = g_ref.shape[2] // rows
    pieces = [x[q, h * rows : (h + 1) * rows] for h in range(per_step) for q in range(blocks)]
    down_ref[...] = jnp.concatenate(pieces, axis=0).astype(down_ref.dtype)


def unpack(gathered, rows):
    kinds_blocks, total, width = gathered.shape
    blocks = kinds_blocks // 3
    g = gathered.reshape(3, blocks, total, width)
    step = 16 * rows
    dt = gathered.dtype
    nbytes = 2 * gathered.size * dt.itemsize
    return pl.pallas_call(
        functools.partial(unpack_kernel, rows),
        grid=(total // step,),
        in_specs=[pl.BlockSpec((3, blocks, step, width), lambda j: (0, 0, j, 0))],
        out_specs=[
            pl.BlockSpec((blocks, step, width), lambda j: (0, j, 0)),
            pl.BlockSpec((step, blocks * width), lambda j: (j, 0)),
            pl.BlockSpec((blocks * step, width), lambda j: (j, 0)),
        ],
        out_shape=[
            jax.ShapeDtypeStruct((blocks, total, width), dt),
            jax.ShapeDtypeStruct((total, blocks * width), dt),
            jax.ShapeDtypeStruct((blocks * total, width), dt),
        ],
        cost_estimate=pl.CostEstimate(flops=0, transcendentals=0, bytes_accessed=nbytes),
    )(g)


def rep_sum(parts):
    n = lax.axis_size("rep")
    me = lax.axis_index("rep")
    held = [parts] + [
        lax.ppermute(parts, "rep", [(i, (i + d) % n) for i in range(n)]) for d in range(1, n)
    ]
    stack = jnp.stack(held)
    by_index = [lax.dynamic_index_in_dim(stack, (me - k) % n, keepdims=False) for k in range(n)]
    while len(by_index) > 1:
        by_index = [a + b for a, b in zip(by_index[::2], by_index[1::2])]
    return by_index[0]


def on_device(
    trained_sq,
    trained_up,
    trained_down,
    trained_ln,
    start_sq,
    start_up,
    start_down,
    start_ln,
    resid_sq,
    resid_up,
    resid_down,
    mom_sq,
    mom_up,
    mom_down,
    mom_ln,
    basis_sq,
    basis_up,
    basis_down,
):
    highest = lax.Precision.HIGHEST
    groups = lax.axis_size("rep")
    square, rows, width = start_sq.shape
    rank = basis_sq.shape[-1]
    delta_sq = start_sq - trained_sq[0] + resid_sq[0]
    factor_sq = jnp.einsum("mrd,mdk->mrk", delta_sq, basis_sq, precision=highest)
    new_resid_sq = delta_sq - jnp.einsum("mrk,mdk->mrd", factor_sq, basis_sq, precision=highest)
    delta_up = start_up - trained_up[0] + resid_up[0]
    factor_up = jnp.dot(delta_up, basis_up, precision=highest, preferred_element_type=jnp.float32)
    new_resid_up = delta_up - jnp.einsum("rk,fk->rf", factor_up, basis_up, precision=highest)
    delta_down = start_down - trained_down[0] + resid_down[0]
    factor_down = jnp.dot(
        delta_down, basis_down, precision=highest, preferred_element_type=jnp.float32
    )
    new_resid_down = delta_down - jnp.einsum(
        "rk,dk->rd", factor_down, basis_down, precision=highest
    )
    norm_delta = start_ln - trained_ln[0]
    norm_flat = norm_delta.reshape(-1)
    norm_rows = -(-norm_flat.shape[0] // rank)
    norm_pad = jnp.pad(norm_flat, (0, norm_rows * rank - norm_flat.shape[0]))
    parts = [factor_sq.reshape(-1, rank), factor_up, factor_down, norm_pad.reshape(norm_rows, rank)]
    summed = rep_sum(jnp.concatenate(parts)) / groups
    cuts = [p.shape[0] for p in parts]
    at = [sum(cuts[:i]) for i in range(len(cuts))]
    mean_sq = summed[at[0] : at[1]].reshape(factor_sq.shape)
    mean_up = summed[at[1] : at[2]]
    mean_down = summed[at[2] : at[3]]
    mean_ln = summed[at[3] :].reshape(-1)[: norm_flat.shape[0]].reshape(norm_delta.shape)
    blocks_up = start_up.shape[1] // width
    blocks_down = start_down.shape[0] // rows
    start_all = jnp.concatenate(
        [start_sq, split_cols(start_up, width), start_down.reshape(blocks_down, rows, width)]
    )
    mom_all = jnp.concatenate(
        [mom_sq, split_cols(mom_up, width), mom_down.reshape(blocks_down, rows, width)]
    )
    mean_all = jnp.concatenate(
        [
            mean_sq,
            jnp.broadcast_to(mean_up[None], (blocks_up, rows, rank)),
            mean_down.reshape(blocks_down, rows, rank),
        ]
    )
    basis_all = jnp.concatenate(
        [
            basis_sq,
            basis_up.reshape(blocks_up, width, rank),
            jnp.broadcast_to(basis_down[None], (blocks_down, width, rank)),
        ]
    )
    outer_all = jnp.einsum("brk,bdk->brd", mean_all, basis_all, precision=highest)
    new_mom_all, owned_all = advance(start_all, mom_all, outer_all)
    new_mom_sq = new_mom_all[:square]
    new_mom_up = join_cols(new_mom_all[square : square + blocks_up])
    new_mom_down = new_mom_all[square + blocks_up :].reshape(-1, width)
    owned_all, mean_ln = lax.optimization_barrier((owned_all, mean_ln))
    new_mom_ln, norm_weights = advance(start_ln, mom_ln, mean_ln)
    gathered = lax.all_gather(owned_all, "shard", axis=1, tiled=True)
    weights_sq, weights_up, weights_down = unpack(gathered, rows)
    weights_ln = lax.all_gather(norm_weights, "shard", axis=1, tiled=True)
    return (
        new_resid_sq[None],
        new_resid_up[None],
        new_resid_down[None],
        new_mom_sq,
        new_mom_up,
        new_mom_down,
        new_mom_ln,
        weights_sq,
        weights_up,
        weights_down,
        weights_ln,
    )


def solution(mesh):
    placed = (
        P("rep", None, "shard", None),
        P("rep", "shard", None),
        P("rep", "shard", None),
        P("rep", None, "shard"),
        P(None, "shard", None),
        P("shard", None),
        P("shard", None),
        P(None, "shard"),
        P("rep", None, "shard", None),
        P("rep", "shard", None),
        P("rep", "shard", None),
        P(None, "shard", None),
        P("shard", None),
        P("shard", None),
        P(None, "shard"),
        P(),
        P(),
        P(),
    )
    return jax.shard_map(
        on_device,
        mesh=mesh,
        in_specs=placed,
        out_specs=(
            P("rep", None, "shard", None),
            P("rep", "shard", None),
            P("rep", "shard", None),
            P(None, "shard", None),
            P("shard", None),
            P("shard", None),
            P(None, "shard"),
            P(),
            P(),
            P(),
            P(),
        ),
        check_vma=False,
    )
```

```python
import functools

import jax
import jax.numpy as jnp
from jax import lax
from jax.experimental import pallas as pl
from jax.sharding import PartitionSpec as P

moment_coef = 0.9
outer_rate = 0.7


def advance(start, moment, outer):
    new_moment = moment_coef * moment + outer
    weights = (start - outer_rate * (outer + moment_coef * new_moment)).astype(jnp.bfloat16)
    return (new_moment, weights)


def split_cols(a, width):
    return a.reshape(a.shape[0], -1, width).transpose(1, 0, 2)


def join_cols(a):
    return a.transpose(1, 0, 2).reshape(a.shape[1], -1)


def unpack_kernel(rows, g_ref, sq_ref, up_ref, down_ref):
    blocks = g_ref.shape[1]
    sq_ref[...] = g_ref[0]
    up_ref[...] = jnp.concatenate([g_ref[1, k] for k in range(blocks)], axis=1)
    x = g_ref[2].astype(jnp.float32)
    per_step = g_ref.shape[2] // rows
    pieces = [x[q, h * rows : (h + 1) * rows] for h in range(per_step) for q in range(blocks)]
    down_ref[...] = jnp.concatenate(pieces, axis=0).astype(down_ref.dtype)


def unpack(gathered, rows):
    kinds_blocks, total, width = gathered.shape
    blocks = kinds_blocks // 3
    g = gathered.reshape(3, blocks, total, width)
    step = 8 * rows
    dt = gathered.dtype
    nbytes = 2 * gathered.size * dt.itemsize
    return pl.pallas_call(
        functools.partial(unpack_kernel, rows),
        grid=(total // step,),
        in_specs=[pl.BlockSpec((3, blocks, step, width), lambda j: (0, 0, j, 0))],
        out_specs=[
            pl.BlockSpec((blocks, step, width), lambda j: (0, j, 0)),
            pl.BlockSpec((step, blocks * width), lambda j: (j, 0)),
            pl.BlockSpec((blocks * step, width), lambda j: (j, 0)),
        ],
        out_shape=[
            jax.ShapeDtypeStruct((blocks, total, width), dt),
            jax.ShapeDtypeStruct((total, blocks * width), dt),
            jax.ShapeDtypeStruct((blocks * total, width), dt),
        ],
        cost_estimate=pl.CostEstimate(flops=0, transcendentals=0, bytes_accessed=nbytes),
    )(g)


def rep_sum(parts):
    n = lax.axis_size("rep")
    me = lax.axis_index("rep")
    held = [parts] + [
        lax.ppermute(parts, "rep", [(i, (i + d) % n) for i in range(n)]) for d in range(1, n)
    ]
    by_index = [lax.select_n((me - k) % n, *held) for k in range(n)]
    while len(by_index) > 1:
        by_index = [a + b for a, b in zip(by_index[::2], by_index[1::2])]
    return by_index[0]


def on_device(
    trained_sq,
    trained_up,
    trained_down,
    trained_ln,
    start_sq,
    start_up,
    start_down,
    start_ln,
    resid_sq,
    resid_up,
    resid_down,
    mom_sq,
    mom_up,
    mom_down,
    mom_ln,
    basis_sq,
    basis_up,
    basis_down,
):
    highest = lax.Precision.HIGHEST
    groups = lax.axis_size("rep")
    square, rows, width = start_sq.shape
    rank = basis_sq.shape[-1]
    delta_sq = start_sq - trained_sq[0] + resid_sq[0]
    factor_sq = jnp.einsum("mrd,mdk->mrk", delta_sq, basis_sq, precision=highest)
    new_resid_sq = delta_sq - jnp.einsum("mrk,mdk->mrd", factor_sq, basis_sq, precision=highest)
    delta_up = start_up - trained_up[0] + resid_up[0]
    factor_up = jnp.dot(delta_up, basis_up, precision=highest, preferred_element_type=jnp.float32)
    new_resid_up = delta_up - jnp.einsum("rk,fk->rf", factor_up, basis_up, precision=highest)
    delta_down = start_down - trained_down[0] + resid_down[0]
    factor_down = jnp.dot(
        delta_down, basis_down, precision=highest, preferred_element_type=jnp.float32
    )
    new_resid_down = delta_down - jnp.einsum(
        "rk,dk->rd", factor_down, basis_down, precision=highest
    )
    norm_delta = start_ln - trained_ln[0]
    norm_flat = norm_delta.reshape(-1)
    norm_rows = -(-norm_flat.shape[0] // rank)
    norm_pad = jnp.pad(norm_flat, (0, norm_rows * rank - norm_flat.shape[0]))
    parts = [factor_sq.reshape(-1, rank), factor_up, factor_down, norm_pad.reshape(norm_rows, rank)]
    summed = rep_sum(jnp.concatenate(parts)) / groups
    cuts = [p.shape[0] for p in parts]
    at = [sum(cuts[:i]) for i in range(len(cuts))]
    mean_sq = summed[at[0] : at[1]].reshape(factor_sq.shape)
    mean_up = summed[at[1] : at[2]]
    mean_down = summed[at[2] : at[3]]
    mean_ln = summed[at[3] :].reshape(-1)[: norm_flat.shape[0]].reshape(norm_delta.shape)
    blocks_up = start_up.shape[1] // width
    blocks_down = start_down.shape[0] // rows
    start_all = jnp.concatenate(
        [start_sq, split_cols(start_up, width), start_down.reshape(blocks_down, rows, width)]
    )
    mom_all = jnp.concatenate(
        [mom_sq, split_cols(mom_up, width), mom_down.reshape(blocks_down, rows, width)]
    )
    mean_all = jnp.concatenate(
        [
            mean_sq,
            jnp.broadcast_to(mean_up[None], (blocks_up, rows, rank)),
            mean_down.reshape(blocks_down, rows, rank),
        ]
    )
    basis_all = jnp.concatenate(
        [
            basis_sq,
            basis_up.reshape(blocks_up, width, rank),
            jnp.broadcast_to(basis_down[None], (blocks_down, width, rank)),
        ]
    )
    outer_all = jnp.einsum("brk,bdk->brd", mean_all, basis_all, precision=highest)
    new_mom_all, owned_all = advance(start_all, mom_all, outer_all)
    new_mom_sq = new_mom_all[:square]
    new_mom_up = join_cols(new_mom_all[square : square + blocks_up])
    new_mom_down = new_mom_all[square + blocks_up :].reshape(-1, width)
    owned_all, mean_ln = lax.optimization_barrier((owned_all, mean_ln))
    new_mom_ln, norm_weights = advance(start_ln, mom_ln, mean_ln)
    gathered = lax.all_gather(owned_all, "shard", axis=1, tiled=True)
    weights_sq, weights_up, weights_down = unpack(gathered, rows)
    weights_ln = lax.all_gather(norm_weights, "shard", axis=1, tiled=True)
    return (
        new_resid_sq[None],
        new_resid_up[None],
        new_resid_down[None],
        new_mom_sq,
        new_mom_up,
        new_mom_down,
        new_mom_ln,
        weights_sq,
        weights_up,
        weights_down,
        weights_ln,
    )


def solution(mesh):
    placed = (
        P("rep", None, "shard", None),
        P("rep", "shard", None),
        P("rep", "shard", None),
        P("rep", None, "shard"),
        P(None, "shard", None),
        P("shard", None),
        P("shard", None),
        P(None, "shard"),
        P("rep", None, "shard", None),
        P("rep", "shard", None),
        P("rep", "shard", None),
        P(None, "shard", None),
        P("shard", None),
        P("shard", None),
        P(None, "shard"),
        P(),
        P(),
        P(),
    )
    return jax.shard_map(
        on_device,
        mesh=mesh,
        in_specs=placed,
        out_specs=(
            P("rep", None, "shard", None),
            P("rep", "shard", None),
            P("rep", "shard", None),
            P(None, "shard", None),
            P("shard", None),
            P("shard", None),
            P(None, "shard"),
            P(),
            P(),
            P(),
            P(),
        ),
        check_vma=False,
    )
```
